256 devices in a mesh: tm: 32 (over x, y, core), row: 8 (over z).
Axes of the slice: x: 4, y: 4, z: 8, core: 2. Of those that a mesh axis runs over, the one named last changes fastest.
Arguments:
- right_side: float32 [32, 512, 1024], P('tm', 'row'), may hold values from -6 to 6
- kappa: float32 [512, 1024], P('row'), may hold values from 0.5 to 8
Outputs:
- solution: float32 [32, 512, 1024], P('tm', 'row')
The draws below stay inside these ranges and needn't reach their ends.
All inputs are finite; a program needn't handle non-finite values.
Results may differ from the reference program's by a relative error of at most 0.0003.
Values sent between devices are 32-bit elements; how exact they have to be, the bound alone decides.
No kernel may reach another device: no remote copies, remote signals or barrier semaphores. Data moves between devices by JAX's collectives and lax.ppermute only.
A program may use at most 64 MiB of HBM per device.

```python
import math
import jax
import jax.numpy as jnp
from jax import lax

NY = 1024
SWEEPS = 2
DEGREE = 4
NT = 32
NX = 512


def block_levels(key, dims, cuts, least, largest):
    def one(dim, parts):
        steps = jax.random.uniform(jax.random.fold_in(jax.random.fold_in(key, 6), dim), (parts,), jnp.float32, least / len(cuts), largest / len(cuts))
        return jnp.repeat(jnp.exp(steps), dims[dim] // parts).reshape((-1,) + (1,) * (len(dims) - dim - 1))

    loudness = one(*cuts[0])
    for cut in cuts[1:]:
        loudness = loudness * one(*cut)
    return loudness


def normal_values(own_key, shape, spread, bound, cuts=(), kind=jnp.bfloat16):
    values = spread * jax.random.normal(own_key, shape, jnp.float32)
    if cuts:
        values = values * block_levels(own_key, shape, cuts, -0.22, 0.18)
    return jnp.clip(values, -bound, bound).astype(kind)


def setup_inputs(seed: int = 0) -> dict:
    key_list = jax.random.split(jax.random.key(seed), 3)
    right_side = normal_values(key_list[0], (NT, NX, NY), 1.0, 6.0, ((0, 32), (1, 8)), jnp.float32)
    kappa = jnp.clip(jnp.exp(math.log(8.0) - 2.7725887 * jax.random.uniform(key_list[1], (NX, NY), jnp.float32) ** block_levels(key_list[1], (NX, NY), ((0, 8),), -0.2, 0.2)), 0.5, 8.0)
    return dict(right_side=right_side, kappa=kappa)


circulant_alpha = 0.05
courant_rows = 0.5
courant_cols = 0.25
cheb_centre = 1.0
cheb_half = 0.7


def step_weights(count):
    return [1.0 / (cheb_centre + cheb_half * math.cos(math.pi * (2 * number + 1) / (2 * count))) for number in range(count)]


def face_terms(kappa):
    padded = jnp.pad(kappa, 1)
    centre = padded[1:-1, 1:-1]
    north = 0.5 * (centre + padded[2:, 1:-1])
    south = 0.5 * (centre + padded[:-2, 1:-1])
    east = 0.5 * (centre + padded[1:-1, 2:])
    west = 0.5 * (centre + padded[1:-1, :-2])
    diagonal = north + south + east + west + (courant_rows + courant_cols)
    return north, south, east, west, diagonal


def spatial(field, faces):
    north, south, east, west, diagonal = faces
    padded = jnp.pad(field, ((0, 0), (1, 1), (1, 1)))
    centre = padded[:, 1:-1, 1:-1]
    above = padded[:, 2:, 1:-1]
    below = padded[:, :-2, 1:-1]
    after = padded[:, 1:-1, 2:]
    before = padded[:, 1:-1, :-2]
    coupled = north * above + south * below + east * after + west * before
    return diagonal * centre - coupled - courant_rows * below - courant_cols * before


def reference(right_side, kappa):
    faces = face_terms(kappa)
    diagonal = faces[4]
    steps = jnp.arange(NT, dtype=jnp.int32).astype(jnp.float32)
    log_alpha = math.log(circulant_alpha)
    scaled = right_side * jnp.exp(log_alpha * steps / NT)[:, None, None]
    spectrum = jnp.fft.fft(scaled, axis=0)
    spec_real = jnp.real(spectrum)
    spec_imag = jnp.imag(spectrum)
    decay = circulant_alpha ** (1.0 / NT)
    weights = step_weights(DEGREE)

    def solve_one(item):
        rhs_real, rhs_imag, frequency = item
        theta = (2.0 * math.pi / NT) * frequency.astype(jnp.float32)
        shift_real = 1.0 - decay * jnp.cos(theta)
        shift_imag = decay * jnp.sin(theta)
        diag_real = shift_real + diagonal
        magnitude = diag_real * diag_real + shift_imag * shift_imag
        inv_real = diag_real / magnitude
        inv_imag = -shift_imag / magnitude
        rhs = jnp.stack([rhs_real, rhs_imag])
        state = jnp.zeros_like(rhs)
        first = True
        for sweep in range(SWEEPS):
            for weight in weights:
                if first:
                    residual = rhs
                    first = False
                else:
                    image = spatial(state, faces)
                    image_real = shift_real * state[0] - shift_imag * state[1] + image[0]
                    image_imag = shift_real * state[1] + shift_imag * state[0] + image[1]
                    residual = rhs - jnp.stack([image_real, image_imag])
                corr_real = inv_real * residual[0] - inv_imag * residual[1]
                corr_imag = inv_real * residual[1] + inv_imag * residual[0]
                state = state + weight * jnp.stack([corr_real, corr_imag])
        return state[0], state[1]

    frequencies = jnp.arange(NT, dtype=jnp.int32)
    sol_real, sol_imag = lax.map(solve_one, (spec_real, spec_imag, frequencies))
    signal = jnp.real(jnp.fft.ifft(sol_real + 1j * sol_imag, axis=0))
    return signal * jnp.exp(-log_alpha * steps / NT)[:, None, None]
```

```python
import math

import jax
import jax.numpy as jnp
from jax import lax
from jax.sharding import PartitionSpec as P

SWEEPS = 2
DEGREE = 4
HALO = 8


circulant_alpha = 0.05
courant_rows = 0.5
courant_cols = 0.25
cheb_centre = 1.0
cheb_half = 0.7


def from_partner(value, axis, bit):
    mask = 2**bit
    pairs = [(source, source ^ mask) for source in range(lax.axis_size(axis))]
    return lax.ppermute(value, axis, pairs)


def step_weights(count):
    return [
        1.0 / (cheb_centre + cheb_half * math.cos(math.pi * (2 * number + 1) / (2 * count)))
        for number in range(count)
    ]


def face_terms(kappa_rows):
    padded = jnp.pad(kappa_rows, ((0, 0), (1, 1)))
    centre = padded[1:-1, 1:-1]
    north = 0.5 * (centre + padded[2:, 1:-1])
    south = 0.5 * (centre + padded[:-2, 1:-1])
    east = 0.5 * (centre + padded[1:-1, 2:])
    west = 0.5 * (centre + padded[1:-1, :-2])
    diagonal = north + south + east + west + (courant_rows + courant_cols)
    return (north, south, east, west, diagonal)


def spatial(extended, faces):
    north, south, east, west, diagonal = faces
    padded = jnp.pad(extended, ((0, 0), (0, 0), (0, 0), (1, 1)))
    centre = padded[:, :, 1:-1, 1:-1]
    above = padded[:, :, 2:, 1:-1]
    below = padded[:, :, :-2, 1:-1]
    after = padded[:, :, 1:-1, 2:]
    before = padded[:, :, 1:-1, :-2]
    coupled = north * above + south * below + east * after + west * before
    return diagonal * centre - coupled - courant_rows * below - courant_cols * before


def rotate(pair, cosine, sine):
    return jnp.stack([pair[0] * cosine - pair[1] * sine, pair[0] * sine + pair[1] * cosine])


def short_transform(pair, sign):
    count = pair.shape[1]
    index = jnp.arange(count, dtype=jnp.int32)
    angles = 2.0 * math.pi / count * (index[:, None] * index[None, :] % count).astype(jnp.float32)
    cosine = jnp.cos(angles)
    sine = sign * jnp.sin(angles)
    highest = lax.Precision.HIGHEST
    real = jnp.einsum("kj,jrc->krc", cosine, pair[0], precision=highest) - jnp.einsum(
        "kj,jrc->krc", sine, pair[1], precision=highest
    )
    imag = jnp.einsum("kj,jrc->krc", cosine, pair[1], precision=highest) + jnp.einsum(
        "kj,jrc->krc", sine, pair[0], precision=highest
    )
    return jnp.stack([real, imag])


def bit_reversed(device, levels):
    total = jnp.zeros((), jnp.int32)
    for place in range(levels):
        total = total + device // 2**place % 2 * 2 ** (levels - 1 - place)
    return total


def forward_pairs(scaled, device, levels, tm_size, total_steps):
    place = levels - 1
    half = 2**place
    lower = device // half % 2 == 1
    angle = -math.pi / half * (device % half).astype(jnp.float32)
    partner = from_partner(scaled, "tm", place)
    summed = scaled + partner
    differ = partner - scaled
    real = jnp.where(lower, differ * jnp.cos(angle), summed)
    imag = jnp.where(lower, differ * jnp.sin(angle), jnp.zeros_like(summed))
    state = jnp.stack([real, imag])
    for place in range(levels - 2, -1, -1):
        half = 2**place
        lower = device // half % 2 == 1
        angle = -math.pi / half * (device % half).astype(jnp.float32)
        partner = from_partner(state, "tm", place)
        summed = state + partner
        rotated = rotate(partner - state, jnp.cos(angle), jnp.sin(angle))
        state = jnp.where(lower, rotated, summed)
    first_index = bit_reversed(device, levels)
    steps_dev = scaled.shape[0]
    local_steps = jnp.arange(steps_dev, dtype=jnp.int32)
    twist = (
        -2.0 * math.pi / total_steps * (local_steps * first_index % total_steps).astype(jnp.float32)
    )
    state = rotate(state, jnp.cos(twist)[:, None, None], jnp.sin(twist)[:, None, None])
    spectrum = short_transform(state, -1.0)
    frequencies = first_index + tm_size * local_steps
    return (spectrum, frequencies)


def backward_pairs(solved, device, levels, total_steps):
    steps_dev = solved.shape[1]
    first_index = bit_reversed(device, levels)
    state = short_transform(solved, 1.0) * (1.0 / steps_dev)
    local_steps = jnp.arange(steps_dev, dtype=jnp.int32)
    twist = (
        2.0 * math.pi / total_steps * (local_steps * first_index % total_steps).astype(jnp.float32)
    )
    state = rotate(state, jnp.cos(twist)[:, None, None], jnp.sin(twist)[:, None, None])
    for place in range(0, levels - 1):
        half = 2**place
        lower = device // half % 2 == 1
        angle = math.pi / half * (device % half).astype(jnp.float32)
        cosine = jnp.cos(angle)
        sine = jnp.sin(angle)
        partner = from_partner(state, "tm", place)
        upper_value = (state + rotate(partner, cosine, sine)) * 0.5
        lower_value = (partner - rotate(state, cosine, sine)) * 0.5
        state = jnp.where(lower, lower_value, upper_value)
    place = levels - 1
    half = 2**place
    lower = device // half % 2 == 1
    angle = math.pi / half * (device % half).astype(jnp.float32)
    own_turned = state[0] * jnp.cos(angle) - state[1] * jnp.sin(angle)
    outgoing = jnp.where(lower, own_turned, state[0])
    received = from_partner(outgoing, "tm", place)
    return jnp.where(lower, (received - own_turned) * 0.5, (state[0] + received) * 0.5)


def shift_terms(frequencies, faces, total_steps):
    decay = circulant_alpha ** (1.0 / total_steps)
    theta = 2.0 * math.pi / total_steps * frequencies.astype(jnp.float32)
    shift_real = (1.0 - decay * jnp.cos(theta))[:, None, None]
    shift_imag = (decay * jnp.sin(theta))[:, None, None]
    diag_real = shift_real + faces[4]
    magnitude = diag_real * diag_real + shift_imag * shift_imag
    return (shift_real, shift_imag, diag_real / magnitude, -shift_imag / magnitude)


def solve_each(spectrum, frequencies, kappa_rows, inside):
    total_steps = spectrum.shape[1] * lax.axis_size("tm")
    faces = face_terms(jnp.pad(kappa_rows, ((1, 1), (0, 0))))
    shift_real, shift_imag, inv_real, inv_imag = shift_terms(frequencies, faces, total_steps)
    inv_real = inv_real * inside
    inv_imag = inv_imag * inside
    state = jnp.zeros_like(spectrum)
    first = True
    for sweep in range(SWEEPS):
        for weight in step_weights(DEGREE):
            if first:
                residual = spectrum
                first = False
            else:
                extended = jnp.pad(state, ((0, 0), (0, 0), (1, 1), (0, 0)))
                image = spatial(extended, faces)
                image_real = shift_real * state[0] - shift_imag * state[1] + image[0]
                image_imag = shift_real * state[1] + shift_imag * state[0] + image[1]
                residual = spectrum - jnp.stack([image_real, image_imag])
            corr_real = inv_real * residual[0] - inv_imag * residual[1]
            corr_imag = inv_real * residual[1] + inv_imag * residual[0]
            state = state + weight * jnp.stack([corr_real, corr_imag])
    return state


def with_halo(right_side, kappa, width):
    rows = kappa.shape[0]
    count = lax.axis_size("row")
    forward = [(i, i + 1) for i in range(count - 1)]
    backward = [(target, source) for source, target in forward]
    joined = jnp.concatenate([right_side, kappa[None]], axis=0)
    low = lax.ppermute(joined[:, rows - width :], "row", forward)
    high = lax.ppermute(joined[:, :width], "row", backward)
    joined = jnp.concatenate([low, joined, high], axis=1)
    place = lax.axis_index("row") * rows - width + jnp.arange(rows + 2 * width)
    inside = ((place >= 0) & (place < rows * count)).astype(jnp.float32)[:, None]
    return joined[:-1], joined[-1], inside


def body(right_side, kappa):
    steps_dev = right_side.shape[0]
    rows = kappa.shape[0]
    width = HALO
    tm_size = lax.axis_size("tm")
    total_steps = steps_dev * tm_size
    device = lax.axis_index("tm")
    local_steps = jnp.arange(steps_dev, dtype=jnp.int32)
    global_steps = device * steps_dev + local_steps
    log_alpha = math.log(circulant_alpha)
    step_float = global_steps.astype(jnp.float32)
    wide_side, kappa_rows, inside = with_halo(right_side, kappa, width)
    scaled = wide_side * jnp.exp(log_alpha * step_float / total_steps)[:, None, None]
    levels = tm_size.bit_length() - 1
    spectrum, frequencies = forward_pairs(scaled, device, levels, tm_size, total_steps)
    solved = solve_each(spectrum, frequencies, kappa_rows, inside)
    solved = solved[:, :, width : width + rows]
    signal = backward_pairs(solved, device, levels, total_steps)
    return signal * jnp.exp(-log_alpha * step_float / total_steps)[:, None, None]


def solution(mesh):
    placed = (P("tm", "row", None), P("row", None))
    return jax.shard_map(
        body, mesh=mesh, in_specs=placed, out_specs=P("tm", "row", None), check_vma=False
    )
```

```python
import math

import jax
import jax.numpy as jnp
import numpy as np
from jax import lax
from jax.sharding import PartitionSpec as P

SWEEPS = 2
DEGREE = 4
HALO = 8


circulant_alpha = 0.05
courant_rows = 0.5
courant_cols = 0.25
cheb_centre = 1.0
cheb_half = 0.7


def step_weights(count):
    return [
        1.0 / (cheb_centre + cheb_half * math.cos(math.pi * (2 * number + 1) / (2 * count)))
        for number in range(count)
    ]


def with_halo(right_side, kappa, width):
    rows = kappa.shape[0]
    count = lax.axis_size("row")
    forward = [(i, i + 1) for i in range(count - 1)]
    backward = [(target, source) for source, target in forward]
    joined = jnp.concatenate([right_side, kappa[None]], axis=0)
    low = lax.ppermute(joined[:, rows - width :], "row", forward)
    high = lax.ppermute(joined[:, :width], "row", backward)
    joined = jnp.concatenate([low, joined, high], axis=1)
    place = lax.axis_index("row") * rows - width + jnp.arange(rows + 2 * width)
    inside = (place >= 0) & (place < rows * count)
    return joined[0], joined[1], inside


def transform_matrices(total):
    half = total // 2
    steps = np.arange(total)
    scale = circulant_alpha ** (steps / total)
    forward = np.zeros((total, total))
    inverse = np.zeros((total, total))
    forward[0] = 1.0
    forward[half] = (-1.0) ** steps
    inverse[:, 0] = 1.0
    inverse[:, half] = (-1.0) ** steps
    for slot in range(1, half):
        angle = 2.0 * np.pi * slot * steps / total
        forward[slot] = np.cos(angle)
        forward[half + slot] = -np.sin(angle)
        inverse[:, slot] = 2.0 * np.cos(angle)
        inverse[:, half + slot] = -2.0 * np.sin(angle)
    forward = forward * scale[None, :]
    inverse = inverse / total / scale[:, None]
    return forward.astype(np.float32), inverse.astype(np.float32)


def slot_shifts(half, total, width):
    decay = circulant_alpha ** (1.0 / total)
    slots = np.arange(half)
    theta = 2.0 * np.pi / total * slots
    real_a = 1.0 - decay * np.cos(theta)
    real_b = real_a.copy()
    imag = decay * np.sin(theta)
    real_b[0] = 1.0 + decay
    imag[0] = 0.0
    spread = lambda v: np.repeat(v.astype(np.float32), width)[None, :]
    return spread(real_a), spread(real_b), spread(imag)


def tile_faces(kappa_rows, tile, tiles, width, margin):
    rows, cols = kappa_rows.shape
    span = cols // tiles
    padded = jnp.pad(kappa_rows, ((1, 1), (margin + 1, width - span - margin + 1)))
    block = lax.dynamic_slice_in_dim(padded, tile * span, width + 2, axis=1)
    centre = block[1:-1, 1:-1]
    north = 0.5 * (centre + block[2:, 1:-1])
    south = 0.5 * (centre + block[:-2, 1:-1])
    east = 0.5 * (centre + block[1:-1, 2:])
    west = 0.5 * (centre + block[1:-1, :-2])
    diagonal = north + south + east + west + (courant_rows + courant_cols)
    return (north, south, east, west, diagonal)


def column_tiles(field, tiles, width, margin):
    rows, cols = field.shape
    span = cols // tiles
    padded = jnp.pad(field, ((0, 0), (margin, 2 * span - margin)))
    main = padded[:, :cols].reshape(rows, tiles, span)
    extra = padded[:, span : cols + span].reshape(rows, tiles, span)[:, :, : width - span]
    return jnp.concatenate([main, extra], axis=2).transpose(1, 0, 2)


def spatial(state, faces):
    north, south, east, west, diagonal = faces
    rows_padded = jnp.pad(state, ((0, 0), (1, 1), (0, 0)))
    cols_padded = jnp.pad(state, ((0, 0), (0, 0), (1, 1)))
    above = rows_padded[:, 2:]
    below = rows_padded[:, :-2]
    after = cols_padded[:, :, 2:]
    before = cols_padded[:, :, :-2]
    coupled = north * above + south * below + east * after + west * before
    return diagonal * state - coupled - courant_rows * below - courant_cols * before


def solve_slots(spectrum, faces, shifts, inside):
    real_a, real_b, imag = shifts
    diag_a = real_a + faces[4]
    diag_b = real_b + faces[4]
    mag_a = diag_a * diag_a + imag * imag
    mag_b = diag_b * diag_b + imag * imag
    inv_a = jnp.where(inside, diag_a / mag_a, 0.0)
    inv_b = jnp.where(inside, diag_b / mag_b, 0.0)
    inv_imag = jnp.where(inside, -imag / mag_a, 0.0)
    state = jnp.zeros_like(spectrum)
    first = True
    for sweep in range(SWEEPS):
        for weight in step_weights(DEGREE):
            if first:
                residual = spectrum
                first = False
            else:
                image = spatial(state, faces)
                image_real = real_a * state[0] - imag * state[1] + image[0]
                image_imag = real_b * state[1] + imag * state[0] + image[1]
                residual = spectrum - jnp.stack([image_real, image_imag])
            corr_real = inv_a * residual[0] - inv_imag * residual[1]
            corr_imag = inv_b * residual[1] + inv_imag * residual[0]
            state = state + weight * jnp.stack([corr_real, corr_imag])
    return state


def body(right_side, kappa):
    steps_dev, rows, cols = right_side.shape
    tiles = lax.axis_size("tm")
    total = steps_dev * tiles
    half = total // 2
    margin = HALO
    span = cols // tiles
    width = span + 2 * margin
    tile = lax.axis_index("tm")
    highest = lax.Precision.HIGHEST
    forward, inverse = transform_matrices(total)

    wide_side, kappa_rows, inside_rows = with_halo(right_side, kappa, margin)
    extended = rows + 2 * margin
    sent = column_tiles(wide_side, tiles, width, margin)
    gathered = lax.all_to_all(sent, "tm", 0, 0, tiled=True)
    spectrum = jnp.einsum("pt,trc->prc", forward, gathered, precision=highest)
    spectrum = spectrum.reshape(2, half, extended, width).transpose(0, 2, 1, 3)
    spectrum = spectrum.reshape(2, extended, half * width)

    place = tile * span - margin + jnp.arange(width)
    inside_cols = (place >= 0) & (place < cols)
    inside = inside_rows[:, None] & inside_cols[None, :]
    inside = jnp.tile(inside, (1, half))
    faces = tuple(jnp.tile(f, (1, half)) for f in tile_faces(kappa_rows, tile, tiles, width, margin))
    shifts = slot_shifts(half, total, width)
    solved = solve_slots(spectrum, faces, shifts, inside)

    solved = solved.reshape(2, extended, half, width)[:, margin : margin + rows, :, margin : margin + span]
    solved = solved.transpose(0, 2, 1, 3).reshape(total, rows, span)
    signal = jnp.einsum("tp,prc->trc", inverse, solved, precision=highest)
    returned = lax.all_to_all(signal, "tm", 0, 0, tiled=True)
    return returned.transpose(1, 0, 2).reshape(steps_dev, rows, cols)


def solution(mesh):
    placed = (P("tm", "row", None), P("row", None))
    return jax.shard_map(
        body, mesh=mesh, in_specs=placed, out_specs=P("tm", "row", None), check_vma=False
    )
```

```python
import math

import jax
import jax.numpy as jnp
import numpy as np
from jax import lax
from jax.experimental import pallas as pl
from jax.experimental.pallas import tpu as pltpu
from jax.sharding import PartitionSpec as P

SWEEPS = 2
DEGREE = 4
HALO = 8


circulant_alpha = 0.05
courant_rows = 0.5
courant_cols = 0.25
cheb_centre = 1.0
cheb_half = 0.7


def step_weights(count):
    return [
        1.0 / (cheb_centre + cheb_half * math.cos(math.pi * (2 * number + 1) / (2 * count)))
        for number in range(count)
    ]


def with_halo(right_side, kappa, width):
    rows = kappa.shape[0]
    count = lax.axis_size("row")
    forward = [(i, i + 1) for i in range(count - 1)]
    backward = [(target, source) for source, target in forward]
    joined = jnp.concatenate([right_side, kappa[None]], axis=0)
    low = lax.ppermute(joined[:, rows - width :], "row", forward)
    high = lax.ppermute(joined[:, :width], "row", backward)
    joined = jnp.concatenate([low, joined, high], axis=1)
    place = lax.axis_index("row") * rows - width + jnp.arange(rows + 2 * width)
    inside = (place >= 0) & (place < rows * count)
    return joined[0], joined[1], inside


def transform_matrices(total):
    half = total // 2
    steps = np.arange(total)
    scale = circulant_alpha ** (steps / total)
    forward = np.zeros((total, total))
    inverse = np.zeros((total, total))
    forward[0] = 1.0
    forward[half] = (-1.0) ** steps
    inverse[:, 0] = 1.0
    inverse[:, half] = (-1.0) ** steps
    for slot in range(1, half):
        angle = 2.0 * np.pi * slot * steps / total
        forward[slot] = np.cos(angle)
        forward[half + slot] = -np.sin(angle)
        inverse[:, slot] = 2.0 * np.cos(angle)
        inverse[:, half + slot] = -2.0 * np.sin(angle)
    forward = forward * scale[None, :]
    inverse = inverse / total / scale[:, None]
    return forward.astype(np.float32), inverse.astype(np.float32)


def slot_shifts(half, total, width):
    decay = circulant_alpha ** (1.0 / total)
    slots = np.arange(half)
    theta = 2.0 * np.pi / total * slots
    real_a = 1.0 - decay * np.cos(theta)
    real_b = real_a.copy()
    imag = decay * np.sin(theta)
    real_b[0] = 1.0 + decay
    imag[0] = 0.0
    spread = lambda v: np.repeat(v.astype(np.float32), width)[None, :]
    return spread(real_a), spread(real_b), spread(imag)


def tile_faces(kappa_rows, tile, tiles, width, margin):
    rows, cols = kappa_rows.shape
    span = cols // tiles
    padded = jnp.pad(kappa_rows, ((1, 1), (margin + 1, width - span - margin + 1)))
    block = lax.dynamic_slice_in_dim(padded, tile * span, width + 2, axis=1)
    centre = block[1:-1, 1:-1]
    north = 0.5 * (centre + block[2:, 1:-1])
    south = 0.5 * (centre + block[:-2, 1:-1])
    east = 0.5 * (centre + block[1:-1, 2:])
    west = 0.5 * (centre + block[1:-1, :-2])
    diagonal = north + south + east + west + (courant_rows + courant_cols)
    return (north, south, east, west, diagonal)


def column_tiles(field, tiles, width, margin):
    rows, cols = field.shape
    span = cols // tiles
    padded = jnp.pad(field, ((0, 0), (margin, 2 * span - margin)))
    main = padded[:, :cols].reshape(rows, tiles, span)
    extra = padded[:, span : cols + span].reshape(rows, tiles, span)[:, :, : width - span]
    return jnp.concatenate([main, extra], axis=2).transpose(1, 0, 2)


def solve_kernel(spec_ref, north_ref, south_ref, east_ref, west_ref, diag_ref,
                 inva_ref, invb_ref, invi_ref, reala_ref, realb_ref, imag_ref, out_ref):
    rows, lanes = north_ref.shape

    def spatial(x):
        above = pltpu.roll(x, rows - 1, 0)
        below = pltpu.roll(x, 1, 0)
        after = pltpu.roll(x, lanes - 1, 1)
        before = pltpu.roll(x, 1, 1)
        coupled = (north_ref[...] * above + south_ref[...] * below
                   + east_ref[...] * after + west_ref[...] * before)
        return diag_ref[...] * x - coupled - courant_rows * below - courant_cols * before

    first = True
    for sweep in range(SWEEPS):
        for weight in step_weights(DEGREE):
            if first:
                res_real = spec_ref[0]
                res_imag = spec_ref[1]
            else:
                state_real = out_ref[0]
                state_imag = out_ref[1]
                image_real = (reala_ref[...] * state_real - imag_ref[...] * state_imag
                              + spatial(state_real))
                image_imag = (realb_ref[...] * state_imag + imag_ref[...] * state_real
                              + spatial(state_imag))
                res_real = spec_ref[0] - image_real
                res_imag = spec_ref[1] - image_imag
            corr_real = inva_ref[...] * res_real - invi_ref[...] * res_imag
            corr_imag = invb_ref[...] * res_imag + invi_ref[...] * res_real
            if first:
                out_ref[0] = weight * corr_real
                out_ref[1] = weight * corr_imag
                first = False
            else:
                out_ref[0] = out_ref[0] + weight * corr_real
                out_ref[1] = out_ref[1] + weight * corr_imag


def solve_slots(spectrum, faces, shifts, inside):
    real_a, real_b, imag = shifts
    diag_a = real_a + faces[4]
    diag_b = real_b + faces[4]
    mag_a = diag_a * diag_a + imag * imag
    mag_b = diag_b * diag_b + imag * imag
    inv_a = jnp.where(inside, diag_a / mag_a, 0.0)
    inv_b = jnp.where(inside, diag_b / mag_b, 0.0)
    inv_imag = jnp.where(inside, -imag / mag_a, 0.0)
    operands = (spectrum,) + tuple(faces) + (inv_a, inv_b, inv_imag) + tuple(
        jnp.asarray(s) for s in shifts
    )
    return pl.pallas_call(
        solve_kernel,
        out_shape=jax.ShapeDtypeStruct(spectrum.shape, spectrum.dtype),
    )(*operands)


def body(right_side, kappa):
    steps_dev, rows, cols = right_side.shape
    tiles = lax.axis_size("tm")
    total = steps_dev * tiles
    half = total // 2
    margin = HALO
    span = cols // tiles
    width = span + 2 * margin
    tile = lax.axis_index("tm")
    highest = lax.Precision.HIGHEST
    forward, inverse = transform_matrices(total)

    wide_side, kappa_rows, inside_rows = with_halo(right_side, kappa, margin)
    extended = rows + 2 * margin
    sent = column_tiles(wide_side, tiles, width, margin)
    gathered = lax.all_to_all(sent, "tm", 0, 0, tiled=True)
    spectrum = jnp.einsum("pt,trc->prc", forward, gathered, precision=highest)
    spectrum = spectrum.reshape(2, half, extended, width).transpose(0, 2, 1, 3)
    spectrum = spectrum.reshape(2, extended, half * width)

    place = tile * span - margin + jnp.arange(width)
    inside_cols = (place >= 0) & (place < cols)
    inside = inside_rows[:, None] & inside_cols[None, :]
    inside = jnp.tile(inside, (1, half))
    faces = tuple(jnp.tile(f, (1, half)) for f in tile_faces(kappa_rows, tile, tiles, width, margin))
    shifts = slot_shifts(half, total, width)
    solved = solve_slots(spectrum, faces, shifts, inside)

    solved = solved.reshape(2, extended, half, width)[:, margin : margin + rows, :, margin : margin + span]
    solved = solved.transpose(0, 2, 1, 3).reshape(total, rows, span)
    signal = jnp.einsum("tp,prc->trc", inverse, solved, precision=highest)
    returned = lax.all_to_all(signal, "tm", 0, 0, tiled=True)
    return returned.transpose(1, 0, 2).reshape(steps_dev, rows, cols)


def solution(mesh):
    placed = (P("tm", "row", None), P("row", None))
    return jax.shard_map(
        body, mesh=mesh, in_specs=placed, out_specs=P("tm", "row", None), check_vma=False
    )
```

```python
import math

import jax
import jax.numpy as jnp
import numpy as np
from jax import lax
from jax.experimental import pallas as pl
from jax.experimental.pallas import tpu as pltpu
from jax.sharding import PartitionSpec as P

SWEEPS = 2
DEGREE = 4
HALO = 8


circulant_alpha = 0.05
courant_rows = 0.5
courant_cols = 0.25
cheb_centre = 1.0
cheb_half = 0.7


def step_weights(count):
    return [
        1.0 / (cheb_centre + cheb_half * math.cos(math.pi * (2 * number + 1) / (2 * count)))
        for number in range(count)
    ]


def row_pairs():
    count = lax.axis_size("row")
    forward = [(i, i + 1) for i in range(count - 1)]
    backward = [(target, source) for source, target in forward]
    return forward, backward


def with_halo(kappa, width):
    rows = kappa.shape[0]
    count = lax.axis_size("row")
    forward, backward = row_pairs()
    low = lax.ppermute(kappa[rows - width :], "row", forward)
    high = lax.ppermute(kappa[:width], "row", backward)
    place = lax.axis_index("row") * rows - width + jnp.arange(rows + 2 * width)
    inside = (place >= 0) & (place < rows * count)
    return jnp.concatenate([low, kappa, high], axis=0), inside


def add_spill(solved, width):
    rows = solved.shape[1] - 2 * width
    forward, backward = row_pairs()
    from_low = lax.ppermute(solved[:, rows + width :], "row", forward)
    from_high = lax.ppermute(solved[:, :width], "row", backward)
    own = solved[:, width : rows + width]
    spill = jnp.concatenate(
        [from_low, jnp.zeros_like(own[:, : rows - 2 * width]), from_high], axis=1
    )
    return own + spill


def transform_matrices(total):
    half = total // 2
    steps = np.arange(total)
    scale = circulant_alpha ** (steps / total)
    forward = np.zeros((total, total))
    inverse = np.zeros((total, total))
    forward[0] = 1.0
    forward[half] = (-1.0) ** steps
    inverse[:, 0] = 1.0
    inverse[:, half] = (-1.0) ** steps
    for slot in range(1, half):
        angle = 2.0 * np.pi * slot * steps / total
        forward[slot] = np.cos(angle)
        forward[half + slot] = -np.sin(angle)
        inverse[:, slot] = 2.0 * np.cos(angle)
        inverse[:, half + slot] = -2.0 * np.sin(angle)
    forward = forward * scale[None, :]
    inverse = inverse / total / scale[:, None]
    return forward.astype(np.float32), inverse.astype(np.float32)


def slot_shifts(half, total, width):
    decay = circulant_alpha ** (1.0 / total)
    slots = np.arange(half)
    theta = 2.0 * np.pi / total * slots
    real_a = 1.0 - decay * np.cos(theta)
    real_b = real_a.copy()
    imag = decay * np.sin(theta)
    real_b[0] = 1.0 + decay
    imag[0] = 0.0
    spread = lambda v: np.repeat(v.astype(np.float32), width)[None, :]
    return spread(real_a), spread(real_b), spread(imag)


def tile_faces(kappa_rows, tile, tiles, width, margin):
    rows, cols = kappa_rows.shape
    span = cols // tiles
    padded = jnp.pad(kappa_rows, ((1, 1), (margin + 1, width - span - margin + 1)))
    block = lax.dynamic_slice_in_dim(padded, tile * span, width + 2, axis=1)
    centre = block[1:-1, 1:-1]
    north = 0.5 * (centre + block[2:, 1:-1])
    south = 0.5 * (centre + block[:-2, 1:-1])
    east = 0.5 * (centre + block[1:-1, 2:])
    west = 0.5 * (centre + block[1:-1, :-2])
    diagonal = north + south + east + west + (courant_rows + courant_cols)
    return (north, south, east, west, diagonal)


def column_tiles(field, tiles, width, margin):
    rows, cols = field.shape
    span = cols // tiles
    padded = jnp.pad(field, ((0, 0), (margin, 2 * span - margin)))
    main = padded[:, :cols].reshape(rows, tiles, span)
    extra = padded[:, span : cols + span].reshape(rows, tiles, span)[:, :, : width - span]
    return jnp.concatenate([main, extra], axis=2).transpose(1, 0, 2)


def solve_kernel(spec_ref, north_ref, south_ref, east_ref, west_ref, diag_ref,
                 inva_ref, invb_ref, invi_ref, reala_ref, realb_ref, imag_ref, out_ref):
    rows, lanes = north_ref.shape

    def spatial(x):
        above = pltpu.roll(x, rows - 1, 0)
        below = pltpu.roll(x, 1, 0)
        after = pltpu.roll(x, lanes - 1, 1)
        before = pltpu.roll(x, 1, 1)
        coupled = (north_ref[...] * above + south_ref[...] * below
                   + east_ref[...] * after + west_ref[...] * before)
        return diag_ref[...] * x - coupled - courant_rows * below - courant_cols * before

    first = True
    for sweep in range(SWEEPS):
        for weight in step_weights(DEGREE):
            if first:
                res_real = spec_ref[0]
                res_imag = spec_ref[1]
            else:
                state_real = out_ref[0]
                state_imag = out_ref[1]
                image_real = (reala_ref[...] * state_real - imag_ref[...] * state_imag
                              + spatial(state_real))
                image_imag = (realb_ref[...] * state_imag + imag_ref[...] * state_real
                              + spatial(state_imag))
                res_real = spec_ref[0] - image_real
                res_imag = spec_ref[1] - image_imag
            corr_real = inva_ref[...] * res_real - invi_ref[...] * res_imag
            corr_imag = invb_ref[...] * res_imag + invi_ref[...] * res_real
            if first:
                out_ref[0] = weight * corr_real
                out_ref[1] = weight * corr_imag
                first = False
            else:
                out_ref[0] = out_ref[0] + weight * corr_real
                out_ref[1] = out_ref[1] + weight * corr_imag


def solve_slots(spectrum, faces, shifts, inside):
    real_a, real_b, imag = shifts
    diag_a = real_a + faces[4]
    diag_b = real_b + faces[4]
    mag_a = diag_a * diag_a + imag * imag
    mag_b = diag_b * diag_b + imag * imag
    inv_a = jnp.where(inside, diag_a / mag_a, 0.0)
    inv_b = jnp.where(inside, diag_b / mag_b, 0.0)
    inv_imag = jnp.where(inside, -imag / mag_a, 0.0)
    operands = (spectrum,) + tuple(faces) + (inv_a, inv_b, inv_imag) + tuple(
        jnp.asarray(s) for s in shifts
    )
    return pl.pallas_call(
        solve_kernel,
        out_shape=jax.ShapeDtypeStruct(spectrum.shape, spectrum.dtype),
    )(*operands)


def body(right_side, kappa):
    steps_dev, rows, cols = right_side.shape
    tiles = lax.axis_size("tm")
    total = steps_dev * tiles
    half = total // 2
    margin = HALO
    span = cols // tiles
    width = span + 2 * margin
    tile = lax.axis_index("tm")
    precision = lax.Precision.HIGH
    forward, inverse = transform_matrices(total)

    kappa_rows, inside_rows = with_halo(kappa, margin)
    extended = rows + 2 * margin
    sent = column_tiles(right_side[0], tiles, width, margin)
    gathered = lax.all_to_all(sent, "tm", 0, 0, tiled=True)
    spectrum = jnp.einsum("pt,trc->prc", forward, gathered, precision=precision)
    spectrum = spectrum.reshape(2, half, rows, width).transpose(0, 2, 1, 3)
    spectrum = spectrum.reshape(2, rows, half * width)
    spectrum = jnp.pad(spectrum, ((0, 0), (margin, margin), (0, 0)))

    place = tile * span - margin + jnp.arange(width)
    inside_cols = (place >= 0) & (place < cols)
    inside = inside_rows[:, None] & inside_cols[None, :]
    inside = jnp.tile(inside, (1, half))
    faces = tuple(jnp.tile(f, (1, half)) for f in tile_faces(kappa_rows, tile, tiles, width, margin))
    shifts = slot_shifts(half, total, width)
    solved = add_spill(solve_slots(spectrum, faces, shifts, inside), margin)

    solved = solved.reshape(2, rows, half, width)[..., margin : margin + span]
    solved = solved.transpose(0, 2, 1, 3).reshape(total, rows * span)
    signal = jnp.dot(inverse, solved, precision=precision)
    returned = lax.all_to_all(signal, "tm", 0, 0, tiled=True)
    returned = returned.reshape(tiles, rows, span).transpose(1, 0, 2)
    return returned.reshape(steps_dev, rows, cols)


def solution(mesh):
    placed = (P("tm", "row", None), P("row", None))
    return jax.shard_map(
        body, mesh=mesh, in_specs=placed, out_specs=P("tm", "row", None), check_vma=False
    )
```

```python
import math

import jax
import jax.numpy as jnp
import numpy as np
from jax import lax
from jax.experimental import pallas as pl
from jax.experimental.pallas import tpu as pltpu
from jax.sharding import PartitionSpec as P

SWEEPS = 2
DEGREE = 4
HALO = 8


circulant_alpha = 0.05
courant_rows = 0.5
courant_cols = 0.25
cheb_centre = 1.0
cheb_half = 0.7


def step_weights(count):
    return [
        1.0 / (cheb_centre + cheb_half * math.cos(math.pi * (2 * number + 1) / (2 * count)))
        for number in range(count)
    ]


def with_halo(right_side, kappa, width):
    rows = kappa.shape[0]
    count = lax.axis_size("row")
    forward = [(i, i + 1) for i in range(count - 1)]
    backward = [(target, source) for source, target in forward]
    joined = jnp.concatenate([right_side, kappa[None]], axis=0)
    low = lax.ppermute(joined[:, rows - width :], "row", forward)
    high = lax.ppermute(joined[:, :width], "row", backward)
    joined = jnp.concatenate([low, joined, high], axis=1)
    place = lax.axis_index("row") * rows - width + jnp.arange(rows + 2 * width)
    inside = (place >= 0) & (place < rows * count)
    return joined[0], joined[1], inside


def transform_matrices(total):
    half = total // 2
    steps = np.arange(total)
    scale = circulant_alpha ** (steps / total)
    forward = np.zeros((total, total))
    inverse = np.zeros((total, total))
    forward[0] = 1.0
    forward[half] = (-1.0) ** steps
    inverse[:, 0] = 1.0
    inverse[:, half] = (-1.0) ** steps
    for slot in range(1, half):
        angle = 2.0 * np.pi * slot * steps / total
        forward[slot] = np.cos(angle)
        forward[half + slot] = -np.sin(angle)
        inverse[:, slot] = 2.0 * np.cos(angle)
        inverse[:, half + slot] = -2.0 * np.sin(angle)
    forward = forward * scale[None, :]
    inverse = inverse / total / scale[:, None]
    return forward.astype(np.float32), inverse.astype(np.float32)


def slot_shifts(half, total, width):
    decay = circulant_alpha ** (1.0 / total)
    slots = np.arange(half)
    theta = 2.0 * np.pi / total * slots
    real_a = 1.0 - decay * np.cos(theta)
    real_b = real_a.copy()
    imag = decay * np.sin(theta)
    real_b[0] = 1.0 + decay
    imag[0] = 0.0
    spread = lambda v: np.repeat(v.astype(np.float32), width)[None, :]
    return spread(real_a), spread(real_b), spread(imag)


def tile_faces(kappa_rows, tile, tiles, width, margin):
    rows, cols = kappa_rows.shape
    span = cols // tiles
    padded = jnp.pad(kappa_rows, ((1, 1), (margin + 1, width - span - margin + 1)))
    block = lax.dynamic_slice_in_dim(padded, tile * span, width + 2, axis=1)
    centre = block[1:-1, 1:-1]
    north = 0.5 * (centre + block[2:, 1:-1])
    south = 0.5 * (centre + block[:-2, 1:-1])
    east = 0.5 * (centre + block[1:-1, 2:])
    west = 0.5 * (centre + block[1:-1, :-2])
    diagonal = north + south + east + west + (courant_rows + courant_cols)
    return (north, south, east, west, diagonal)


def column_tiles(field, tiles, width, margin):
    rows, cols = field.shape
    span = cols // tiles
    padded = jnp.pad(field, ((0, 0), (margin, 2 * span - margin)))
    main = padded[:, :cols].reshape(rows, tiles, span)
    extra = padded[:, span : cols + span].reshape(rows, tiles, span)[:, :, : width - span]
    return jnp.concatenate([main, extra], axis=2).transpose(1, 0, 2)


def solve_kernel(spec_ref, north_ref, south_ref, east_ref, west_ref, diag_ref,
                 inva_ref, invb_ref, invi_ref, reala_ref, realb_ref, imag_ref, out_ref):
    rows, lanes = north_ref.shape

    def spatial(x):
        above = pltpu.roll(x, rows - 1, 0)
        below = pltpu.roll(x, 1, 0)
        after = pltpu.roll(x, lanes - 1, 1)
        before = pltpu.roll(x, 1, 1)
        coupled = (north_ref[...] * above + south_ref[...] * below
                   + east_ref[...] * after + west_ref[...] * before)
        return diag_ref[...] * x - coupled - courant_rows * below - courant_cols * before

    first = True
    for sweep in range(SWEEPS):
        for weight in step_weights(DEGREE):
            if first:
                res_real = spec_ref[0]
                res_imag = spec_ref[1]
            else:
                state_real = out_ref[0]
                state_imag = out_ref[1]
                image_real = (reala_ref[...] * state_real - imag_ref[...] * state_imag
                              + spatial(state_real))
                image_imag = (realb_ref[...] * state_imag + imag_ref[...] * state_real
                              + spatial(state_imag))
                res_real = spec_ref[0] - image_real
                res_imag = spec_ref[1] - image_imag
            corr_real = inva_ref[...] * res_real - invi_ref[...] * res_imag
            corr_imag = invb_ref[...] * res_imag + invi_ref[...] * res_real
            if first:
                out_ref[0] = weight * corr_real
                out_ref[1] = weight * corr_imag
                first = False
            else:
                out_ref[0] = out_ref[0] + weight * corr_real
                out_ref[1] = out_ref[1] + weight * corr_imag


def solve_slots(spectrum, faces, shifts, inside):
    real_a, real_b, imag = shifts
    diag_a = real_a + faces[4]
    diag_b = real_b + faces[4]
    mag_a = diag_a * diag_a + imag * imag
    mag_b = diag_b * diag_b + imag * imag
    inv_a = jnp.where(inside, diag_a / mag_a, 0.0)
    inv_b = jnp.where(inside, diag_b / mag_b, 0.0)
    inv_imag = jnp.where(inside, -imag / mag_a, 0.0)
    operands = (spectrum,) + tuple(faces) + (inv_a, inv_b, inv_imag) + tuple(
        jnp.asarray(s) for s in shifts
    )
    return pl.pallas_call(
        solve_kernel,
        out_shape=jax.ShapeDtypeStruct(spectrum.shape, spectrum.dtype),
    )(*operands)


def body(right_side, kappa):
    steps_dev, rows, cols = right_side.shape
    tiles = lax.axis_size("tm")
    total = steps_dev * tiles
    half = total // 2
    margin = HALO
    span = cols // tiles
    width = span + 2 * margin
    tile = lax.axis_index("tm")
    highest = lax.Precision.HIGHEST
    forward, inverse = transform_matrices(total)

    wide_side, kappa_rows, inside_rows = with_halo(right_side, kappa, margin)
    extended = rows + 2 * margin
    sent = column_tiles(wide_side, tiles, width, margin).reshape(tiles, extended * width)
    gathered = lax.all_to_all(sent, "tm", 0, 0, tiled=True)
    spectrum = jnp.dot(forward, gathered, precision=highest)
    spectrum = spectrum.reshape(2, half, extended, width).transpose(0, 2, 1, 3)
    spectrum = spectrum.reshape(2, extended, half * width)

    place = tile * span - margin + jnp.arange(width)
    inside_cols = (place >= 0) & (place < cols)
    inside = inside_rows[:, None] & inside_cols[None, :]
    inside = jnp.tile(inside, (1, half))
    faces = tuple(jnp.tile(f, (1, half)) for f in tile_faces(kappa_rows, tile, tiles, width, margin))
    shifts = slot_shifts(half, total, width)
    solved = solve_slots(spectrum, faces, shifts, inside)

    solved = solved.reshape(2, extended, half, width)[:, margin : margin + rows, :, margin : margin + span]
    solved = solved.transpose(0, 2, 1, 3).reshape(total, rows * span)
    signal = jnp.dot(inverse, solved, precision=highest)
    returned = lax.all_to_all(signal, "tm", 0, 0, tiled=True)
    returned = returned.reshape(tiles, rows, span).transpose(1, 0, 2)
    return returned.reshape(steps_dev, rows, cols)


def solution(mesh):
    placed = (P("tm", "row", None), P("row", None))
    return jax.shard_map(
        body, mesh=mesh, in_specs=placed, out_specs=P("tm", "row", None), check_vma=False
    )
```

```python
import functools
import math

import jax
import jax.numpy as jnp
import numpy as np
from jax import lax
from jax.experimental import pallas as pl
from jax.experimental.pallas import tpu as pltpu
from jax.sharding import PartitionSpec as P

SWEEPS = 2
DEGREE = 4
HALO = 8


circulant_alpha = 0.05
courant_rows = 0.5
courant_cols = 0.25
cheb_centre = 1.0
cheb_half = 0.7


def step_weights(count):
    return [
        1.0 / (cheb_centre + cheb_half * math.cos(math.pi * (2 * number + 1) / (2 * count)))
        for number in range(count)
    ]


def with_halo(right_side, kappa, width):
    rows = kappa.shape[0]
    count = lax.axis_size("row")
    forward = [(i, i + 1) for i in range(count - 1)]
    backward = [(target, source) for source, target in forward]
    joined = jnp.concatenate([right_side, kappa[None]], axis=0)
    low = lax.ppermute(joined[:, rows - width :], "row", forward)
    high = lax.ppermute(joined[:, :width], "row", backward)
    joined = jnp.concatenate([low, joined, high], axis=1)
    place = lax.axis_index("row") * rows - width + jnp.arange(rows + 2 * width)
    inside = (place >= 0) & (place < rows * count)
    return joined[0], joined[1], inside


def transform_matrices(total):
    half = total // 2
    steps = np.arange(total)
    scale = circulant_alpha ** (steps / total)
    forward = np.zeros((total, total))
    inverse = np.zeros((total, total))
    forward[0] = 1.0
    forward[half] = (-1.0) ** steps
    inverse[:, 0] = 1.0
    inverse[:, half] = (-1.0) ** steps
    for slot in range(1, half):
        angle = 2.0 * np.pi * slot * steps / total
        forward[slot] = np.cos(angle)
        forward[half + slot] = -np.sin(angle)
        inverse[:, slot] = 2.0 * np.cos(angle)
        inverse[:, half + slot] = -2.0 * np.sin(angle)
    forward = forward * scale[None, :]
    inverse = inverse / total / scale[:, None]
    return forward.astype(np.float32), inverse.astype(np.float32)


def slot_shifts(half, total):
    decay = circulant_alpha ** (1.0 / total)
    slots = np.arange(half)
    theta = 2.0 * np.pi / total * slots
    real_a = 1.0 - decay * np.cos(theta)
    real_b = real_a.copy()
    imag = decay * np.sin(theta)
    real_b[0] = 1.0 + decay
    imag[0] = 0.0
    column = lambda v: v.astype(np.float32)[:, None]
    return column(real_a), column(real_b), column(imag)


def tile_faces(kappa_rows, tile, tiles, width, margin):
    rows, cols = kappa_rows.shape
    span = cols // tiles
    padded = jnp.pad(kappa_rows, ((1, 1), (margin + 1, width - span - margin + 1)))
    block = lax.dynamic_slice_in_dim(padded, tile * span, width + 2, axis=1)
    centre = block[1:-1, 1:-1]
    north = 0.5 * (centre + block[2:, 1:-1])
    south = 0.5 * (centre + block[:-2, 1:-1])
    east = 0.5 * (centre + block[1:-1, 2:])
    west = 0.5 * (centre + block[1:-1, :-2])
    diagonal = north + south + east + west + (courant_rows + courant_cols)
    return (north, south, east, west, diagonal)


def column_tiles(field, tiles, width, margin):
    rows, cols = field.shape
    span = cols // tiles
    padded = jnp.pad(field, ((0, 0), (margin, 2 * span - margin)))
    main = padded[:, :cols].reshape(rows, tiles, span)
    extra = padded[:, span : cols + span].reshape(rows, tiles, span)[:, :, : width - span]
    return jnp.concatenate([main, extra], axis=2).transpose(1, 0, 2)


def solve_kernel(step, spec_ref, north_ref, south_ref, east_ref, west_ref, diag_a_ref, diag_b_ref,
                 imag_ref, inva_ref, invb_ref, invi_ref, out_ref):
    group = north_ref.shape[0]
    half, lanes = inva_ref.shape

    def coupled(x):
        above = pltpu.roll(x, lanes - step, 1)
        below = pltpu.roll(x, step, 1)
        after = pltpu.roll(x, lanes - 1, 1)
        before = pltpu.roll(x, 1, 1)
        return (north_ref[...] * above + south_ref[...] * below + east_ref[...] * after
                + west_ref[...] * before + courant_rows * below + courant_cols * before)

    for start in range(0, half, group):
        part = slice(start, start + group)
        real = slice(start, start + group)
        imag = slice(half + start, half + start + group)
        first = True
        for sweep in range(SWEEPS):
            for weight in step_weights(DEGREE):
                if first:
                    res_real = spec_ref[real]
                    res_imag = spec_ref[imag]
                else:
                    state_real = out_ref[real]
                    state_imag = out_ref[imag]
                    image_real = (diag_a_ref[part] * state_real - imag_ref[part] * state_imag
                                  - coupled(state_real))
                    image_imag = (diag_b_ref[part] * state_imag + imag_ref[part] * state_real
                                  - coupled(state_imag))
                    res_real = spec_ref[real] - image_real
                    res_imag = spec_ref[imag] - image_imag
                corr_real = inva_ref[part] * res_real - invi_ref[part] * res_imag
                corr_imag = invb_ref[part] * res_imag + invi_ref[part] * res_real
                if first:
                    out_ref[real] = weight * corr_real
                    out_ref[imag] = weight * corr_imag
                    first = False
                else:
                    out_ref[real] = out_ref[real] + weight * corr_real
                    out_ref[imag] = out_ref[imag] + weight * corr_imag


def solve_slots(spectrum, faces, shifts, inside, width):
    real_a, real_b, imag = shifts
    group = 8
    north, south, east, west, diagonal = (f.reshape(1, -1) for f in faces)
    inside = inside.reshape(1, -1)
    diag_a = real_a + diagonal
    diag_b = real_b + diagonal
    mag_a = diag_a * diag_a + imag * imag
    mag_b = diag_b * diag_b + imag * imag
    inv_a = jnp.where(inside, diag_a / mag_a, 0.0)
    inv_b = jnp.where(inside, diag_b / mag_b, 0.0)
    inv_imag = jnp.where(inside, -imag / mag_a, 0.0)
    imag = jnp.broadcast_to(imag, inv_a.shape)
    lanes = north.shape[1]
    spread = lambda f: jnp.broadcast_to(f, (group, lanes))
    operands = (spectrum,) + tuple(spread(f) for f in (north, south, east, west)) + (
        diag_a, diag_b, imag, inv_a, inv_b, inv_imag)
    return pl.pallas_call(
        functools.partial(solve_kernel, width),
        out_shape=jax.ShapeDtypeStruct(spectrum.shape, spectrum.dtype),
    )(*operands)


def body(right_side, kappa):
    steps_dev, rows, cols = right_side.shape
    tiles = lax.axis_size("tm")
    total = steps_dev * tiles
    half = total // 2
    margin = HALO
    span = cols // tiles
    width = span + 2 * margin
    tile = lax.axis_index("tm")
    highest = lax.Precision.HIGHEST
    forward, inverse = transform_matrices(total)

    wide_side, kappa_rows, inside_rows = with_halo(right_side, kappa, margin)
    extended = rows + 2 * margin
    sent = column_tiles(wide_side, tiles, width, margin).reshape(tiles, extended * width)
    gathered = lax.all_to_all(sent, "tm", 0, 0, tiled=True)
    spectrum = jnp.dot(forward, gathered, precision=highest)

    place = tile * span - margin + jnp.arange(width)
    inside_cols = (place >= 0) & (place < cols)
    inside = inside_rows[:, None] & inside_cols[None, :]
    faces = tile_faces(kappa_rows, tile, tiles, width, margin)
    solved = solve_slots(spectrum, faces, slot_shifts(half, total), inside, width)

    signal = jnp.dot(inverse, solved, precision=highest)
    signal = signal.reshape(total, extended, width)[:, margin : margin + rows, margin : margin + span]
    returned = lax.all_to_all(signal.reshape(total, rows * span), "tm", 0, 0, tiled=True)
    returned = returned.reshape(tiles, rows, span).transpose(1, 0, 2)
    return returned.reshape(steps_dev, rows, cols)


def solution(mesh):
    placed = (P("tm", "row", None), P("row", None))
    return jax.shard_map(
        body, mesh=mesh, in_specs=placed, out_specs=P("tm", "row", None), check_vma=False
    )
```

```python
import math

import jax
import jax.numpy as jnp
import numpy as np
from jax import lax
from jax.experimental import pallas as pl
from jax.experimental.pallas import tpu as pltpu
from jax.sharding import PartitionSpec as P

SWEEPS = 2
DEGREE = 4
HALO = 8


circulant_alpha = 0.05
courant_rows = 0.5
courant_cols = 0.25
cheb_centre = 1.0
cheb_half = 0.7


def step_weights(count):
    return [
        1.0 / (cheb_centre + cheb_half * math.cos(math.pi * (2 * number + 1) / (2 * count)))
        for number in range(count)
    ]


def with_halo(right_side, kappa, width):
    rows = kappa.shape[0]
    count = lax.axis_size("row")
    forward = [(i, i + 1) for i in range(count - 1)]
    backward = [(target, source) for source, target in forward]
    joined = jnp.concatenate([right_side, kappa[None]], axis=0)
    low = lax.ppermute(joined[:, rows - width :], "row", forward)
    high = lax.ppermute(joined[:, :width], "row", backward)
    joined = jnp.concatenate([low, joined, high], axis=1)
    place = lax.axis_index("row") * rows - width + jnp.arange(rows + 2 * width)
    inside = (place >= 0) & (place < rows * count)
    return joined[0], joined[1], inside


def transform_matrices(total):
    half = total // 2
    steps = np.arange(total)
    scale = circulant_alpha ** (steps / total)
    forward = np.zeros((total, total))
    inverse = np.zeros((total, total))
    forward[0] = 1.0
    forward[half] = (-1.0) ** steps
    inverse[:, 0] = 1.0
    inverse[:, half] = (-1.0) ** steps
    for slot in range(1, half):
        angle = 2.0 * np.pi * slot * steps / total
        forward[slot] = np.cos(angle)
        forward[half + slot] = -np.sin(angle)
        inverse[:, slot] = 2.0 * np.cos(angle)
        inverse[:, half + slot] = -2.0 * np.sin(angle)
    forward = forward * scale[None, :]
    inverse = inverse / total / scale[:, None]
    return forward.astype(np.float32), inverse.astype(np.float32)


def slot_shifts(half, total, width):
    decay = circulant_alpha ** (1.0 / total)
    slots = np.arange(half)
    theta = 2.0 * np.pi / total * slots
    real_a = 1.0 - decay * np.cos(theta)
    real_b = real_a.copy()
    imag = decay * np.sin(theta)
    real_b[0] = 1.0 + decay
    imag[0] = 0.0
    spread = lambda v: np.repeat(v.astype(np.float32), width)[None, :]
    return spread(real_a), spread(real_b), spread(imag)


def tile_faces(kappa_rows, tile, tiles, width, margin):
    rows, cols = kappa_rows.shape
    span = cols // tiles
    padded = jnp.pad(kappa_rows, ((1, 1), (margin + 1, width - span - margin + 1)))
    block = lax.dynamic_slice_in_dim(padded, tile * span, width + 2, axis=1)
    centre = block[1:-1, 1:-1]
    north = 0.5 * (centre + block[2:, 1:-1])
    south = 0.5 * (centre + block[:-2, 1:-1])
    east = 0.5 * (centre + block[1:-1, 2:])
    west = 0.5 * (centre + block[1:-1, :-2])
    diagonal = north + south + east + west + (courant_rows + courant_cols)
    return (north, south, east, west, diagonal)


def column_tiles(field, tiles, width, margin):
    rows, cols = field.shape
    span = cols // tiles
    padded = jnp.pad(field, ((0, 0), (margin, 2 * span - margin)))
    main = padded[:, :cols].reshape(rows, tiles, span)
    extra = padded[:, span : cols + span].reshape(rows, tiles, span)[:, :, : width - span]
    return jnp.concatenate([main, extra], axis=2).transpose(1, 0, 2)


def solve_kernel(spec_ref, north_ref, south_ref, east_ref, west_ref, diag_ref,
                 inva_ref, invb_ref, invi_ref, reala_ref, realb_ref, imag_ref, out_ref):
    rows, lanes = north_ref.shape

    def spatial(x):
        above = pltpu.roll(x, rows - 1, 0)
        below = pltpu.roll(x, 1, 0)
        after = pltpu.roll(x, lanes - 1, 1)
        before = pltpu.roll(x, 1, 1)
        coupled = (north_ref[...] * above + south_ref[...] * below
                   + east_ref[...] * after + west_ref[...] * before)
        return diag_ref[...] * x - coupled - courant_rows * below - courant_cols * before

    first = True
    for sweep in range(SWEEPS):
        for weight in step_weights(DEGREE):
            if first:
                res_real = spec_ref[0]
                res_imag = spec_ref[1]
            else:
                state_real = out_ref[0]
                state_imag = out_ref[1]
                image_real = (reala_ref[...] * state_real - imag_ref[...] * state_imag
                              + spatial(state_real))
                image_imag = (realb_ref[...] * state_imag + imag_ref[...] * state_real
                              + spatial(state_imag))
                res_real = spec_ref[0] - image_real
                res_imag = spec_ref[1] - image_imag
            corr_real = inva_ref[...] * res_real - invi_ref[...] * res_imag
            corr_imag = invb_ref[...] * res_imag + invi_ref[...] * res_real
            if first:
                out_ref[0] = weight * corr_real
                out_ref[1] = weight * corr_imag
                first = False
            else:
                out_ref[0] = out_ref[0] + weight * corr_real
                out_ref[1] = out_ref[1] + weight * corr_imag


def solve_slots(spectrum, faces, shifts, inside):
    real_a, real_b, imag = shifts
    diag_a = real_a + faces[4]
    diag_b = real_b + faces[4]
    mag_a = diag_a * diag_a + imag * imag
    mag_b = diag_b * diag_b + imag * imag
    inv_a = jnp.where(inside, diag_a / mag_a, 0.0)
    inv_b = jnp.where(inside, diag_b / mag_b, 0.0)
    inv_imag = jnp.where(inside, -imag / mag_a, 0.0)
    operands = (spectrum,) + tuple(faces) + (inv_a, inv_b, inv_imag) + tuple(
        jnp.asarray(s) for s in shifts
    )
    return pl.pallas_call(
        solve_kernel,
        out_shape=jax.ShapeDtypeStruct(spectrum.shape, spectrum.dtype),
    )(*operands)


def body(right_side, kappa):
    steps_dev, rows, cols = right_side.shape
    tiles = lax.axis_size("tm")
    total = steps_dev * tiles
    half = total // 2
    margin = HALO
    span = cols // tiles
    width = span + 2 * margin
    tile = lax.axis_index("tm")
    highest = lax.Precision.HIGHEST
    forward, inverse = transform_matrices(total)

    wide_side, kappa_rows, inside_rows = with_halo(right_side, kappa, margin)
    extended = rows + 2 * margin
    lane = 128
    sent = column_tiles(wide_side, tiles, width, margin).reshape(tiles, -1, lane)
    gathered = lax.all_to_all(sent, "tm", 0, 0, tiled=True).reshape(tiles, extended * width)
    spectrum = jnp.dot(forward, gathered, precision=highest)
    spectrum = spectrum.reshape(2, half, extended, width).transpose(0, 2, 1, 3)
    spectrum = spectrum.reshape(2, extended, half * width)

    place = tile * span - margin + jnp.arange(width)
    inside_cols = (place >= 0) & (place < cols)
    inside = inside_rows[:, None] & inside_cols[None, :]
    inside = jnp.tile(inside, (1, half))
    faces = tuple(jnp.tile(f, (1, half)) for f in tile_faces(kappa_rows, tile, tiles, width, margin))
    shifts = slot_shifts(half, total, width)
    solved = solve_slots(spectrum, faces, shifts, inside)

    solved = solved.reshape(2, extended, half, width)[:, margin : margin + rows, :, margin : margin + span]
    solved = solved.transpose(0, 2, 1, 3).reshape(total, rows * span)
    signal = jnp.dot(inverse, solved, precision=highest)
    signal = signal.reshape(total, -1, lane)
    returned = lax.all_to_all(signal, "tm", 0, 0, tiled=True)
    returned = returned.reshape(tiles, rows, span).transpose(1, 0, 2)
    return returned.reshape(steps_dev, rows, cols)


def solution(mesh):
    placed = (P("tm", "row", None), P("row", None))
    return jax.shard_map(
        body, mesh=mesh, in_specs=placed, out_specs=P("tm", "row", None), check_vma=False
    )
```

```python
import math

import jax
import jax.numpy as jnp
import numpy as np
from jax import lax
from jax.experimental import pallas as pl
from jax.experimental.pallas import tpu as pltpu
from jax.sharding import PartitionSpec as P

SWEEPS = 2
DEGREE = 4
HALO = 8


circulant_alpha = 0.05
courant_rows = 0.5
courant_cols = 0.25
cheb_centre = 1.0
cheb_half = 0.7


def step_weights(count):
    return [
        1.0 / (cheb_centre + cheb_half * math.cos(math.pi * (2 * number + 1) / (2 * count)))
        for number in range(count)
    ]


def with_halo(right_side, kappa, width):
    rows = kappa.shape[0]
    count = lax.axis_size("row")
    forward = [(i, i + 1) for i in range(count - 1)]
    backward = [(target, source) for source, target in forward]
    joined = jnp.concatenate([right_side, kappa[None]], axis=0)
    low = lax.ppermute(joined[:, rows - width :], "row", forward)
    high = lax.ppermute(joined[:, :width], "row", backward)
    joined = jnp.concatenate([low, joined, high], axis=1)
    place = lax.axis_index("row") * rows - width + jnp.arange(rows + 2 * width)
    inside = (place >= 0) & (place < rows * count)
    return joined[0], joined[1], inside


def transform_matrices(total):
    half = total // 2
    steps = np.arange(total)
    scale = circulant_alpha ** (steps / total)
    forward = np.zeros((total, total))
    inverse = np.zeros((total, total))
    forward[0] = 1.0
    forward[half] = (-1.0) ** steps
    inverse[:, 0] = 1.0
    inverse[:, half] = (-1.0) ** steps
    for slot in range(1, half):
        angle = 2.0 * np.pi * slot * steps / total
        forward[slot] = np.cos(angle)
        forward[half + slot] = -np.sin(angle)
        inverse[:, slot] = 2.0 * np.cos(angle)
        inverse[:, half + slot] = -2.0 * np.sin(angle)
    forward = forward * scale[None, :]
    inverse = inverse / total / scale[:, None]
    return forward.astype(np.float32), inverse.astype(np.float32)


def slot_shifts(half, total, width):
    decay = circulant_alpha ** (1.0 / total)
    slots = np.arange(half)
    theta = 2.0 * np.pi / total * slots
    real_a = 1.0 - decay * np.cos(theta)
    real_b = real_a.copy()
    imag = decay * np.sin(theta)
    real_b[0] = 1.0 + decay
    imag[0] = 0.0
    spread = lambda v: np.repeat(v.astype(np.float32), width)[None, :]
    return spread(real_a), spread(real_b), spread(imag)


def tile_faces(kappa_rows, tile, tiles, width, margin):
    rows, cols = kappa_rows.shape
    span = cols // tiles
    padded = jnp.pad(kappa_rows, ((1, 1), (margin + 1, width - span - margin + 1)))
    block = lax.dynamic_slice_in_dim(padded, tile * span, width + 2, axis=1)
    centre = block[1:-1, 1:-1]
    north = 0.5 * (centre + block[2:, 1:-1])
    south = 0.5 * (centre + block[:-2, 1:-1])
    east = 0.5 * (centre + block[1:-1, 2:])
    west = 0.5 * (centre + block[1:-1, :-2])
    diagonal = north + south + east + west + (courant_rows + courant_cols)
    return (north, south, east, west, diagonal)


def column_tiles(field, tiles, width, margin):
    rows, cols = field.shape
    span = cols // tiles
    padded = jnp.pad(field, ((0, 0), (margin, 2 * span - margin)))
    main = padded[:, :cols].reshape(rows, tiles, span)
    extra = padded[:, span : cols + span].reshape(rows, tiles, span)[:, :, : width - span]
    return jnp.concatenate([main, extra], axis=2).transpose(1, 0, 2)


def solve_kernel(spec_ref, north_ref, south_ref, east_ref, west_ref, diag_a_ref, diag_b_ref,
                 inva_ref, invb_ref, invi_ref, imag_ref, out_ref):
    rows, lanes = north_ref.shape

    def coupled(x):
        above = pltpu.roll(x, rows - 1, 0)
        below = pltpu.roll(x, 1, 0)
        after = pltpu.roll(x, lanes - 1, 1)
        before = pltpu.roll(x, 1, 1)
        return (north_ref[...] * above + south_ref[...] * below
                + east_ref[...] * after + west_ref[...] * before)

    first = True
    for sweep in range(SWEEPS):
        for weight in step_weights(DEGREE):
            if first:
                res_real = spec_ref[0]
                res_imag = spec_ref[1]
            else:
                state_real = out_ref[0]
                state_imag = out_ref[1]
                image_real = (diag_a_ref[...] * state_real - imag_ref[...] * state_imag
                              - coupled(state_real))
                image_imag = (diag_b_ref[...] * state_imag + imag_ref[...] * state_real
                              - coupled(state_imag))
                res_real = spec_ref[0] - image_real
                res_imag = spec_ref[1] - image_imag
            corr_real = inva_ref[...] * res_real - invi_ref[...] * res_imag
            corr_imag = invb_ref[...] * res_imag + invi_ref[...] * res_real
            if first:
                out_ref[0] = weight * corr_real
                out_ref[1] = weight * corr_imag
                first = False
            else:
                out_ref[0] = out_ref[0] + weight * corr_real
                out_ref[1] = out_ref[1] + weight * corr_imag


def solve_slots(spectrum, faces, shifts, inside):
    north, south, east, west, diagonal = faces
    real_a, real_b, imag = shifts
    diag_a = real_a + diagonal
    diag_b = real_b + diagonal
    mag_a = diag_a * diag_a + imag * imag
    mag_b = diag_b * diag_b + imag * imag
    inv_a = jnp.where(inside, diag_a / mag_a, 0.0)
    inv_b = jnp.where(inside, diag_b / mag_b, 0.0)
    inv_imag = jnp.where(inside, -imag / mag_a, 0.0)
    operands = (spectrum, north, south + courant_rows, east, west + courant_cols,
                diag_a, diag_b, inv_a, inv_b, inv_imag, jnp.asarray(imag))
    return pl.pallas_call(
        solve_kernel,
        out_shape=jax.ShapeDtypeStruct(spectrum.shape, spectrum.dtype),
    )(*operands)


def body(right_side, kappa):
    steps_dev, rows, cols = right_side.shape
    tiles = lax.axis_size("tm")
    total = steps_dev * tiles
    half = total // 2
    margin = HALO
    span = cols // tiles
    width = span + 2 * margin
    tile = lax.axis_index("tm")
    highest = lax.Precision.HIGHEST
    forward, inverse = transform_matrices(total)

    wide_side, kappa_rows, inside_rows = with_halo(right_side, kappa, margin)
    extended = rows + 2 * margin
    lane = 128
    sent = column_tiles(wide_side, tiles, width, margin).reshape(tiles, -1, lane)
    gathered = lax.all_to_all(sent, "tm", 0, 0, tiled=True).reshape(tiles, extended * width)
    spectrum = jnp.dot(forward, gathered, precision=highest)
    spectrum = spectrum.reshape(2, half, extended, width).transpose(0, 2, 1, 3)
    spectrum = spectrum.reshape(2, extended, half * width)

    place = tile * span - margin + jnp.arange(width)
    inside_cols = (place >= 0) & (place < cols)
    inside = inside_rows[:, None] & inside_cols[None, :]
    inside = jnp.tile(inside, (1, half))
    faces = tuple(jnp.tile(f, (1, half)) for f in tile_faces(kappa_rows, tile, tiles, width, margin))
    shifts = slot_shifts(half, total, width)
    solved = solve_slots(spectrum, faces, shifts, inside)

    solved = solved.reshape(2, extended, half, width)[:, margin : margin + rows, :, margin : margin + span]
    solved = solved.transpose(0, 2, 1, 3).reshape(total, rows * span)
    signal = jnp.dot(inverse, solved, precision=highest)
    signal = signal.reshape(total, -1, lane)
    returned = lax.all_to_all(signal, "tm", 0, 0, tiled=True)
    returned = returned.reshape(tiles, rows, span).transpose(1, 0, 2)
    return returned.reshape(steps_dev, rows, cols)


def solution(mesh):
    placed = (P("tm", "row", None), P("row", None))
    return jax.shard_map(
        body, mesh=mesh, in_specs=placed, out_specs=P("tm", "row", None), check_vma=False
    )
```

```python
import math

import jax
import jax.numpy as jnp
import numpy as np
from jax import lax
from jax.experimental import pallas as pl
from jax.experimental.pallas import tpu as pltpu
from jax.sharding import PartitionSpec as P

SWEEPS = 2
DEGREE = 4
HALO = 8


circulant_alpha = 0.05
courant_rows = 0.5
courant_cols = 0.25
cheb_centre = 1.0
cheb_half = 0.7


def step_weights(count):
    return [
        1.0 / (cheb_centre + cheb_half * math.cos(math.pi * (2 * number + 1) / (2 * count)))
        for number in range(count)
    ]


def with_halo(right_side, kappa, width):
    rows = kappa.shape[0]
    count = lax.axis_size("row")
    forward = [(i, i + 1) for i in range(count - 1)]
    backward = [(target, source) for source, target in forward]
    joined = jnp.concatenate([right_side, kappa[None]], axis=0)
    low = lax.ppermute(joined[:, rows - width :], "row", forward)
    high = lax.ppermute(joined[:, :width], "row", backward)
    joined = jnp.concatenate([low, joined, high], axis=1)
    place = lax.axis_index("row") * rows - width + jnp.arange(rows + 2 * width)
    inside = (place >= 0) & (place < rows * count)
    return joined[0], joined[1], inside


def transform_matrices(total):
    half = total // 2
    steps = np.arange(total)
    scale = circulant_alpha ** (steps / total)
    forward = np.zeros((total, total))
    inverse = np.zeros((total, total))
    forward[0] = 1.0
    forward[half] = (-1.0) ** steps
    inverse[:, 0] = 1.0
    inverse[:, half] = (-1.0) ** steps
    for slot in range(1, half):
        angle = 2.0 * np.pi * slot * steps / total
        forward[slot] = np.cos(angle)
        forward[half + slot] = -np.sin(angle)
        inverse[:, slot] = 2.0 * np.cos(angle)
        inverse[:, half + slot] = -2.0 * np.sin(angle)
    forward = forward * scale[None, :]
    inverse = inverse / total / scale[:, None]
    return forward.astype(np.float32), inverse.astype(np.float32)


def slot_shifts(half, total, width):
    decay = circulant_alpha ** (1.0 / total)
    slots = np.arange(half)
    theta = 2.0 * np.pi / total * slots
    real_a = 1.0 - decay * np.cos(theta)
    real_b = real_a.copy()
    imag = decay * np.sin(theta)
    real_b[0] = 1.0 + decay
    imag[0] = 0.0
    spread = lambda v: np.repeat(v.astype(np.float32), width)[None, :]
    return spread(real_a), spread(real_b), spread(imag)


def tile_faces(kappa_rows, tile, tiles, width, margin):
    rows, cols = kappa_rows.shape
    span = cols // tiles
    padded = jnp.pad(kappa_rows, ((1, 1), (margin + 1, width - span - margin + 1)))
    block = lax.dynamic_slice_in_dim(padded, tile * span, width + 2, axis=1)
    centre = block[1:-1, 1:-1]
    north = 0.5 * (centre + block[2:, 1:-1])
    south = 0.5 * (centre + block[:-2, 1:-1])
    east = 0.5 * (centre + block[1:-1, 2:])
    west = 0.5 * (centre + block[1:-1, :-2])
    diagonal = north + south + east + west + (courant_rows + courant_cols)
    return (north, south, east, west, diagonal)


def column_tiles(field, tiles, width, margin):
    rows, cols = field.shape
    span = cols // tiles
    padded = jnp.pad(field, ((0, 0), (margin, 2 * span - margin)))
    main = padded[:, :cols].reshape(rows, tiles, span)
    extra = padded[:, span : cols + span].reshape(rows, tiles, span)[:, :, : width - span]
    return jnp.concatenate([main, extra], axis=2).transpose(1, 0, 2)


def solve_kernel(spec_ref, north_ref, south_ref, east_ref, west_ref, diag_a_ref, diag_b_ref,
                 inva_ref, invb_ref, invi_ref, imag_ref, out_ref):
    rows, lanes = north_ref.shape

    def coupled(x):
        above = pltpu.roll(x, rows - 1, 0)
        below = pltpu.roll(x, 1, 0)
        after = pltpu.roll(x, lanes - 1, 1)
        before = pltpu.roll(x, 1, 1)
        return (north_ref[...] * above + south_ref[...] * below
                + east_ref[...] * after + west_ref[...] * before)

    first = True
    for sweep in range(SWEEPS):
        for weight in step_weights(DEGREE):
            if first:
                res_real = spec_ref[0]
                res_imag = spec_ref[1]
            else:
                state_real = out_ref[0]
                state_imag = out_ref[1]
                image_real = (diag_a_ref[...] * state_real - imag_ref[...] * state_imag
                              - coupled(state_real))
                image_imag = (diag_b_ref[...] * state_imag + imag_ref[...] * state_real
                              - coupled(state_imag))
                res_real = spec_ref[0] - image_real
                res_imag = spec_ref[1] - image_imag
            corr_real = inva_ref[...] * res_real - invi_ref[...] * res_imag
            corr_imag = invb_ref[...] * res_imag + invi_ref[...] * res_real
            if first:
                out_ref[0] = weight * corr_real
                out_ref[1] = weight * corr_imag
                first = False
            else:
                out_ref[0] = out_ref[0] + weight * corr_real
                out_ref[1] = out_ref[1] + weight * corr_imag


def solve_slots(spectrum, faces, shifts, inside):
    north, south, east, west, diagonal = faces
    real_a, real_b, imag = shifts
    diag_a = real_a + diagonal
    diag_b = real_b + diagonal
    mag_a = diag_a * diag_a + imag * imag
    mag_b = diag_b * diag_b + imag * imag
    inv_a = jnp.where(inside, diag_a / mag_a, 0.0)
    inv_b = jnp.where(inside, diag_b / mag_b, 0.0)
    inv_imag = jnp.where(inside, -imag / mag_a, 0.0)
    operands = (spectrum, north, south + courant_rows, east, west + courant_cols,
                diag_a, diag_b, inv_a, inv_b, inv_imag, jnp.asarray(imag))
    return pl.pallas_call(
        solve_kernel,
        out_shape=jax.ShapeDtypeStruct(spectrum.shape, spectrum.dtype),
    )(*operands)


def body(right_side, kappa):
    steps_dev, rows, cols = right_side.shape
    tiles = lax.axis_size("tm")
    total = steps_dev * tiles
    half = total // 2
    margin = HALO
    span = cols // tiles
    width = span + 2 * margin
    tile = lax.axis_index("tm")
    highest = lax.Precision.HIGHEST
    forward, inverse = transform_matrices(total)

    wide_side, kappa_rows, inside_rows = with_halo(right_side, kappa, margin)
    lane = 128
    tiled = column_tiles(wide_side, tiles, width, margin)

    place = tile * span - margin + jnp.arange(width)
    inside_cols = (place >= 0) & (place < cols)
    inside = jnp.tile(inside_rows[:, None] & inside_cols[None, :], (1, half))
    faces = tuple(jnp.tile(f, (1, half)) for f in tile_faces(kappa_rows, tile, tiles, width, margin))
    shifts = slot_shifts(half, total, width)

    stages = 2
    inner = rows // stages
    depth = inner + 2 * margin
    sent = [tiled[:, s * inner : s * inner + depth].reshape(tiles, -1, lane) for s in range(stages)]
    gathered = [lax.all_to_all(x, "tm", 0, 0, tiled=True) for x in sent]
    outputs = []
    for s in range(stages):
        window = slice(s * inner, s * inner + depth)
        spectrum = jnp.dot(forward, gathered[s].reshape(tiles, depth * width), precision=highest)
        spectrum = spectrum.reshape(2, half, depth, width).transpose(0, 2, 1, 3)
        spectrum = spectrum.reshape(2, depth, half * width)
        solved = solve_slots(
            spectrum, tuple(f[window] for f in faces), shifts, inside[window]
        )
        solved = solved.reshape(2, depth, half, width)[:, margin : margin + inner, :, margin : margin + span]
        solved = solved.transpose(0, 2, 1, 3).reshape(total, inner * span)
        signal = jnp.dot(inverse, solved, precision=highest).reshape(total, -1, lane)
        returned = lax.all_to_all(signal, "tm", 0, 0, tiled=True)
        outputs.append(returned.reshape(tiles, inner, span))
    returned = jnp.concatenate(outputs, axis=1).transpose(1, 0, 2)
    return returned.reshape(steps_dev, rows, cols)


def solution(mesh):
    placed = (P("tm", "row", None), P("row", None))
    return jax.shard_map(
        body, mesh=mesh, in_specs=placed, out_specs=P("tm", "row", None), check_vma=False
    )
```

```python
import math

import jax
import jax.numpy as jnp
import numpy as np
from jax import lax
from jax.experimental import pallas as pl
from jax.experimental.pallas import tpu as pltpu
from jax.sharding import PartitionSpec as P

SWEEPS = 2
DEGREE = 4
HALO = 8


circulant_alpha = 0.05
courant_rows = 0.5
courant_cols = 0.25
cheb_centre = 1.0
cheb_half = 0.7


def step_weights(count):
    return [
        1.0 / (cheb_centre + cheb_half * math.cos(math.pi * (2 * number + 1) / (2 * count)))
        for number in range(count)
    ]


def with_halo(right_side, kappa, width):
    rows = kappa.shape[0]
    count = lax.axis_size("row")
    forward = [(i, i + 1) for i in range(count - 1)]
    backward = [(target, source) for source, target in forward]
    bottom = jnp.stack([right_side[0, rows - width :], kappa[rows - width :]])
    top = jnp.stack([right_side[0, :width], kappa[:width]])
    bottom, top = lax.optimization_barrier((bottom, top))
    low = lax.ppermute(bottom, "row", forward)
    high = lax.ppermute(top, "row", backward)
    joined = jnp.concatenate([right_side, kappa[None]], axis=0)
    joined = jnp.concatenate([low, joined, high], axis=1)
    place = lax.axis_index("row") * rows - width + jnp.arange(rows + 2 * width)
    inside = (place >= 0) & (place < rows * count)
    return joined[0], joined[1], inside


def transform_matrices(total):
    half = total // 2
    steps = np.arange(total)
    scale = circulant_alpha ** (steps / total)
    forward = np.zeros((total, total))
    inverse = np.zeros((total, total))
    forward[0] = 1.0
    forward[half] = (-1.0) ** steps
    inverse[:, 0] = 1.0
    inverse[:, half] = (-1.0) ** steps
    for slot in range(1, half):
        angle = 2.0 * np.pi * slot * steps / total
        forward[slot] = np.cos(angle)
        forward[half + slot] = -np.sin(angle)
        inverse[:, slot] = 2.0 * np.cos(angle)
        inverse[:, half + slot] = -2.0 * np.sin(angle)
    forward = forward * scale[None, :]
    inverse = inverse / total / scale[:, None]
    return forward.astype(np.float32), inverse.astype(np.float32)


def slot_shifts(half, total, width):
    decay = circulant_alpha ** (1.0 / total)
    slots = np.arange(half)
    theta = 2.0 * np.pi / total * slots
    real_a = 1.0 - decay * np.cos(theta)
    real_b = real_a.copy()
    imag = decay * np.sin(theta)
    real_b[0] = 1.0 + decay
    imag[0] = 0.0
    spread = lambda v: np.repeat(v.astype(np.float32), width)[None, :]
    return spread(real_a), spread(real_b), spread(imag)


def tile_faces(kappa_rows, tile, tiles, width, margin):
    rows, cols = kappa_rows.shape
    span = cols // tiles
    padded = jnp.pad(kappa_rows, ((1, 1), (margin + 1, width - span - margin + 1)))
    block = lax.dynamic_slice_in_dim(padded, tile * span, width + 2, axis=1)
    centre = block[1:-1, 1:-1]
    north = 0.5 * (centre + block[2:, 1:-1])
    south = 0.5 * (centre + block[:-2, 1:-1])
    east = 0.5 * (centre + block[1:-1, 2:])
    west = 0.5 * (centre + block[1:-1, :-2])
    diagonal = north + south + east + west + (courant_rows + courant_cols)
    return (north, south, east, west, diagonal)


def column_tiles(field, tiles, width, margin):
    rows, cols = field.shape
    span = cols // tiles
    padded = jnp.pad(field, ((0, 0), (margin, 2 * span - margin)))
    main = padded[:, :cols].reshape(rows, tiles, span)
    extra = padded[:, span : cols + span].reshape(rows, tiles, span)[:, :, : width - span]
    return jnp.concatenate([main, extra], axis=2).transpose(1, 0, 2)


def solve_kernel(spec_ref, north_ref, south_ref, east_ref, west_ref, diag_a_ref, diag_b_ref,
                 inva_ref, invb_ref, invi_ref, imag_ref, out_ref):
    rows, lanes = north_ref.shape

    def coupled(x):
        above = pltpu.roll(x, rows - 1, 0)
        below = pltpu.roll(x, 1, 0)
        after = pltpu.roll(x, lanes - 1, 1)
        before = pltpu.roll(x, 1, 1)
        return (north_ref[...] * above + south_ref[...] * below
                + east_ref[...] * after + west_ref[...] * before)

    first = True
    for sweep in range(SWEEPS):
        for weight in step_weights(DEGREE):
            if first:
                res_real = spec_ref[0]
                res_imag = spec_ref[1]
            else:
                state_real = out_ref[0]
                state_imag = out_ref[1]
                image_real = (diag_a_ref[...] * state_real - imag_ref[...] * state_imag
                              - coupled(state_real))
                image_imag = (diag_b_ref[...] * state_imag + imag_ref[...] * state_real
                              - coupled(state_imag))
                res_real = spec_ref[0] - image_real
                res_imag = spec_ref[1] - image_imag
            corr_real = inva_ref[...] * res_real - invi_ref[...] * res_imag
            corr_imag = invb_ref[...] * res_imag + invi_ref[...] * res_real
            if first:
                out_ref[0] = weight * corr_real
                out_ref[1] = weight * corr_imag
                first = False
            else:
                out_ref[0] = out_ref[0] + weight * corr_real
                out_ref[1] = out_ref[1] + weight * corr_imag


def solve_slots(spectrum, faces, shifts, inside):
    north, south, east, west, diagonal = faces
    real_a, real_b, imag = shifts
    diag_a = real_a + diagonal
    diag_b = real_b + diagonal
    mag_a = diag_a * diag_a + imag * imag
    mag_b = diag_b * diag_b + imag * imag
    inv_a = jnp.where(inside, diag_a / mag_a, 0.0)
    inv_b = jnp.where(inside, diag_b / mag_b, 0.0)
    inv_imag = jnp.where(inside, -imag / mag_a, 0.0)
    operands = (spectrum, north, south + courant_rows, east, west + courant_cols,
                diag_a, diag_b, inv_a, inv_b, inv_imag, jnp.asarray(imag))
    return pl.pallas_call(
        solve_kernel,
        out_shape=jax.ShapeDtypeStruct(spectrum.shape, spectrum.dtype),
    )(*operands)


def body(right_side, kappa):
    steps_dev, rows, cols = right_side.shape
    tiles = lax.axis_size("tm")
    total = steps_dev * tiles
    half = total // 2
    margin = HALO
    span = cols // tiles
    width = span + 2 * margin
    tile = lax.axis_index("tm")
    highest = lax.Precision.HIGHEST
    forward, inverse = transform_matrices(total)

    wide_side, kappa_rows, inside_rows = with_halo(right_side, kappa, margin)
    extended = rows + 2 * margin
    lane = 128
    sent = column_tiles(wide_side, tiles, width, margin).reshape(tiles, -1, lane)
    gathered = lax.all_to_all(sent, "tm", 0, 0, tiled=True).reshape(tiles, extended * width)
    spectrum = jnp.dot(forward, gathered, precision=highest)
    spectrum = spectrum.reshape(2, half, extended, width).transpose(0, 2, 1, 3)
    spectrum = spectrum.reshape(2, extended, half * width)

    place = tile * span - margin + jnp.arange(width)
    inside_cols = (place >= 0) & (place < cols)
    inside = inside_rows[:, None] & inside_cols[None, :]
    inside = jnp.tile(inside, (1, half))
    faces = tuple(jnp.tile(f, (1, half)) for f in tile_faces(kappa_rows, tile, tiles, width, margin))
    shifts = slot_shifts(half, total, width)
    solved = solve_slots(spectrum, faces, shifts, inside)

    solved = solved.reshape(2, extended, half, width)[:, margin : margin + rows, :, margin : margin + span]
    solved = solved.transpose(0, 2, 1, 3).reshape(total, rows * span)
    signal = jnp.dot(inverse, solved, precision=highest)
    signal = signal.reshape(total, -1, lane)
    returned = lax.all_to_all(signal, "tm", 0, 0, tiled=True)
    returned = returned.reshape(tiles, rows, span).transpose(1, 0, 2)
    return returned.reshape(steps_dev, rows, cols)


def solution(mesh):
    placed = (P("tm", "row", None), P("row", None))
    return jax.shard_map(
        body, mesh=mesh, in_specs=placed, out_specs=P("tm", "row", None), check_vma=False
    )
```

```python
import functools
import math

import jax
import jax.numpy as jnp
import numpy as np
from jax import lax
from jax.experimental import pallas as pl
from jax.experimental.pallas import tpu as pltpu
from jax.sharding import PartitionSpec as P

SWEEPS = 2
DEGREE = 4
HALO = 8


circulant_alpha = 0.05
courant_rows = 0.5
courant_cols = 0.25
cheb_centre = 1.0
cheb_half = 0.7


def step_weights(count):
    return [
        1.0 / (cheb_centre + cheb_half * math.cos(math.pi * (2 * number + 1) / (2 * count)))
        for number in range(count)
    ]


def with_halo(right_side, kappa, width):
    rows = kappa.shape[0]
    count = lax.axis_size("row")
    forward = [(i, i + 1) for i in range(count - 1)]
    backward = [(target, source) for source, target in forward]
    bottom = jnp.stack([right_side[0, rows - width :], kappa[rows - width :]])
    top = jnp.stack([right_side[0, :width], kappa[:width]])
    bottom, top = lax.optimization_barrier((bottom, top))
    low = lax.ppermute(bottom, "row", forward)
    high = lax.ppermute(top, "row", backward)
    joined = jnp.concatenate([right_side, kappa[None]], axis=0)
    joined = jnp.concatenate([low, joined, high], axis=1)
    place = lax.axis_index("row") * rows - width + jnp.arange(rows + 2 * width)
    inside = (place >= 0) & (place < rows * count)
    return joined[0], joined[1], inside


def transform_matrices(total):
    half = total // 2
    steps = np.arange(total)
    scale = circulant_alpha ** (steps / total)
    forward = np.zeros((total, total))
    inverse = np.zeros((total, total))
    forward[0] = 1.0
    forward[half] = (-1.0) ** steps
    inverse[:, 0] = 1.0
    inverse[:, half] = (-1.0) ** steps
    for slot in range(1, half):
        angle = 2.0 * np.pi * slot * steps / total
        forward[slot] = np.cos(angle)
        forward[half + slot] = -np.sin(angle)
        inverse[:, slot] = 2.0 * np.cos(angle)
        inverse[:, half + slot] = -2.0 * np.sin(angle)
    forward = forward * scale[None, :]
    inverse = inverse / total / scale[:, None]
    return forward.astype(np.float32), inverse.astype(np.float32)


def slot_shifts(half, total, width):
    decay = circulant_alpha ** (1.0 / total)
    slots = np.arange(half)
    theta = 2.0 * np.pi / total * slots
    real_a = 1.0 - decay * np.cos(theta)
    real_b = real_a.copy()
    imag = decay * np.sin(theta)
    real_b[0] = 1.0 + decay
    imag[0] = 0.0
    spread = lambda v: np.repeat(v.astype(np.float32), width)[None, :]
    return spread(real_a), spread(real_b), spread(imag)


def tile_faces(kappa_rows, tile, tiles, width, margin):
    rows, cols = kappa_rows.shape
    span = cols // tiles
    padded = jnp.pad(kappa_rows, ((1, 1), (margin + 1, width - span - margin + 1)))
    block = lax.dynamic_slice_in_dim(padded, tile * span, width + 2, axis=1)
    centre = block[1:-1, 1:-1]
    north = 0.5 * (centre + block[2:, 1:-1])
    south = 0.5 * (centre + block[:-2, 1:-1])
    east = 0.5 * (centre + block[1:-1, 2:])
    west = 0.5 * (centre + block[1:-1, :-2])
    diagonal = north + south + east + west + (courant_rows + courant_cols)
    return (north, south, east, west, diagonal)


def column_tiles(field, tiles, width, margin):
    rows, cols = field.shape
    span = cols // tiles
    padded = jnp.pad(field, ((0, 0), (margin, 2 * span - margin)))
    main = padded[:, :cols].reshape(rows, tiles, span)
    extra = padded[:, span : cols + span].reshape(rows, tiles, span)[:, :, : width - span]
    return jnp.concatenate([main, extra], axis=2).transpose(1, 0, 2)


def solve_kernel(margin, slabs_ref, north_ref, south_ref, east_ref, west_ref, diag_a_ref,
                 diag_b_ref, inva_ref, invb_ref, invi_ref, imag_ref, interior_ref, spec_ref, out_ref):
    rows, lanes = north_ref.shape
    parts, half, inner, span = interior_ref.shape
    width = lanes // half
    for part in range(parts):
        spec_ref[part] = jnp.concatenate([slabs_ref[part, slot] for slot in range(half)], axis=1)

    def coupled(x):
        above = pltpu.roll(x, rows - 1, 0)
        below = pltpu.roll(x, 1, 0)
        after = pltpu.roll(x, lanes - 1, 1)
        before = pltpu.roll(x, 1, 1)
        return (north_ref[...] * above + south_ref[...] * below
                + east_ref[...] * after + west_ref[...] * before)

    first = True
    for sweep in range(SWEEPS):
        for weight in step_weights(DEGREE):
            if first:
                res_real = spec_ref[0]
                res_imag = spec_ref[1]
            else:
                state_real = out_ref[0]
                state_imag = out_ref[1]
                image_real = (diag_a_ref[...] * state_real - imag_ref[...] * state_imag
                              - coupled(state_real))
                image_imag = (diag_b_ref[...] * state_imag + imag_ref[...] * state_real
                              - coupled(state_imag))
                res_real = spec_ref[0] - image_real
                res_imag = spec_ref[1] - image_imag
            corr_real = inva_ref[...] * res_real - invi_ref[...] * res_imag
            corr_imag = invb_ref[...] * res_imag + invi_ref[...] * res_real
            if first:
                out_ref[0] = weight * corr_real
                out_ref[1] = weight * corr_imag
                first = False
            else:
                out_ref[0] = out_ref[0] + weight * corr_real
                out_ref[1] = out_ref[1] + weight * corr_imag
    for part in range(parts):
        for slot in range(half):
            start = slot * width + margin
            interior_ref[part, slot] = out_ref[part, margin : margin + inner, start : start + span]


def solve_slots(slabs, faces, shifts, inside, rows, span, margin):
    north, south, east, west, diagonal = faces
    real_a, real_b, imag = shifts
    diag_a = real_a + diagonal
    diag_b = real_b + diagonal
    mag_a = diag_a * diag_a + imag * imag
    mag_b = diag_b * diag_b + imag * imag
    inv_a = jnp.where(inside, diag_a / mag_a, 0.0)
    inv_b = jnp.where(inside, diag_b / mag_b, 0.0)
    inv_imag = jnp.where(inside, -imag / mag_a, 0.0)
    operands = (slabs, north, south + courant_rows, east, west + courant_cols,
                diag_a, diag_b, inv_a, inv_b, inv_imag, jnp.asarray(imag))
    parts, half = slabs.shape[:2]
    field = (parts,) + north.shape
    return pl.pallas_call(
        functools.partial(solve_kernel, margin),
        out_shape=jax.ShapeDtypeStruct((parts, half, rows, span), slabs.dtype),
        scratch_shapes=[pltpu.VMEM(field, jnp.float32), pltpu.VMEM(field, jnp.float32)],
    )(*operands)


def body(right_side, kappa):
    steps_dev, rows, cols = right_side.shape
    tiles = lax.axis_size("tm")
    total = steps_dev * tiles
    half = total // 2
    margin = HALO
    span = cols // tiles
    width = span + 2 * margin
    tile = lax.axis_index("tm")
    highest = lax.Precision.HIGHEST
    forward, inverse = transform_matrices(total)

    wide_side, kappa_rows, inside_rows = with_halo(right_side, kappa, margin)
    extended = rows + 2 * margin
    lane = 128
    sent = column_tiles(wide_side, tiles, width, margin).reshape(tiles, -1, lane)
    gathered = lax.all_to_all(sent, "tm", 0, 0, tiled=True).reshape(tiles, extended * width)
    spectrum = jnp.dot(forward, gathered, precision=highest)
    spectrum = spectrum.reshape(2, half, extended, width)

    place = tile * span - margin + jnp.arange(width)
    inside_cols = (place >= 0) & (place < cols)
    inside = inside_rows[:, None] & inside_cols[None, :]
    inside = jnp.tile(inside, (1, half))
    faces = tuple(jnp.tile(f, (1, half)) for f in tile_faces(kappa_rows, tile, tiles, width, margin))
    shifts = slot_shifts(half, total, width)
    solved = solve_slots(spectrum, faces, shifts, inside, rows, span, margin)
    solved = solved.reshape(total, rows * span)
    signal = jnp.dot(inverse, solved, precision=highest)
    signal = signal.reshape(total, -1, lane)
    returned = lax.all_to_all(signal, "tm", 0, 0, tiled=True)
    returned = returned.reshape(tiles, rows, span).transpose(1, 0, 2)
    return returned.reshape(steps_dev, rows, cols)


def solution(mesh):
    placed = (P("tm", "row", None), P("row", None))
    return jax.shard_map(
        body, mesh=mesh, in_specs=placed, out_specs=P("tm", "row", None), check_vma=False
    )
```

```python
import math

import jax
import jax.numpy as jnp
import numpy as np
from jax import lax
from jax.experimental import pallas as pl
from jax.experimental.pallas import tpu as pltpu
from jax.sharding import PartitionSpec as P

SWEEPS = 2
DEGREE = 4
HALO = 8


circulant_alpha = 0.05
courant_rows = 0.5
courant_cols = 0.25
cheb_centre = 1.0
cheb_half = 0.7


def step_weights(count):
    return [
        1.0 / (cheb_centre + cheb_half * math.cos(math.pi * (2 * number + 1) / (2 * count)))
        for number in range(count)
    ]


def with_halo(right_side, kappa, width):
    rows = kappa.shape[0]
    count = lax.axis_size("row")
    forward = [(i, i + 1) for i in range(count - 1)]
    backward = [(target, source) for source, target in forward]
    bottom = jnp.stack([right_side[0, rows - width :], kappa[rows - width :]])
    top = jnp.stack([right_side[0, :width], kappa[:width]])
    bottom, top = lax.optimization_barrier((bottom, top))
    low = lax.ppermute(bottom, "row", forward)
    high = lax.ppermute(top, "row", backward)
    joined = jnp.concatenate([right_side, kappa[None]], axis=0)
    joined = jnp.concatenate([low, joined, high], axis=1)
    place = lax.axis_index("row") * rows - width + jnp.arange(rows + 2 * width)
    inside = (place >= 0) & (place < rows * count)
    return joined[0], joined[1], inside


def core_pairs(count):
    return [(source, source ^ 1) for source in range(count)]


def chip_groups(count):
    return [[2 * chip + core for chip in range(count // 2)] for core in range(2)]


def gather_steps(sent):
    count = sent.shape[0]
    core = lax.axis_index("tm") % 2
    pairs = sent.reshape((count // 2, 2) + sent.shape[1:])
    keep = jnp.where(core == 0, pairs[:, 0], pairs[:, 1])
    give = jnp.where(core == 0, pairs[:, 1], pairs[:, 0])
    got = lax.ppermute(give, "tm", core_pairs(count))
    both = jnp.where(core == 0, jnp.stack([keep, got], 1), jnp.stack([got, keep], 1))
    received = lax.all_to_all(both, "tm", 0, 0, axis_index_groups=chip_groups(count), tiled=True)
    return received.reshape(sent.shape)


def scatter_steps(signal):
    count = signal.shape[0]
    core = lax.axis_index("tm") % 2
    pairs = signal.reshape((count // 2, 2) + signal.shape[1:])
    received = lax.all_to_all(pairs, "tm", 0, 0, axis_index_groups=chip_groups(count), tiled=True)
    mine = jnp.where(core == 0, received[:, 0], received[:, 1])
    other = jnp.where(core == 0, received[:, 1], received[:, 0])
    got = lax.ppermute(other, "tm", core_pairs(count))
    both = jnp.where(core == 0, jnp.stack([mine, got], 1), jnp.stack([got, mine], 1))
    return both.reshape(signal.shape)


def transform_matrices(total):
    half = total // 2
    steps = np.arange(total)
    scale = circulant_alpha ** (steps / total)
    forward = np.zeros((total, total))
    inverse = np.zeros((total, total))
    forward[0] = 1.0
    forward[half] = (-1.0) ** steps
    inverse[:, 0] = 1.0
    inverse[:, half] = (-1.0) ** steps
    for slot in range(1, half):
        angle = 2.0 * np.pi * slot * steps / total
        forward[slot] = np.cos(angle)
        forward[half + slot] = -np.sin(angle)
        inverse[:, slot] = 2.0 * np.cos(angle)
        inverse[:, half + slot] = -2.0 * np.sin(angle)
    forward = forward * scale[None, :]
    inverse = inverse / total / scale[:, None]
    return forward.astype(np.float32), inverse.astype(np.float32)


def slot_shifts(half, total, width):
    decay = circulant_alpha ** (1.0 / total)
    slots = np.arange(half)
    theta = 2.0 * np.pi / total * slots
    real_a = 1.0 - decay * np.cos(theta)
    real_b = real_a.copy()
    imag = decay * np.sin(theta)
    real_b[0] = 1.0 + decay
    imag[0] = 0.0
    spread = lambda v: np.repeat(v.astype(np.float32), width)[None, :]
    return spread(real_a), spread(real_b), spread(imag)


def tile_faces(kappa_rows, tile, tiles, width, margin):
    rows, cols = kappa_rows.shape
    span = cols // tiles
    padded = jnp.pad(kappa_rows, ((1, 1), (margin + 1, width - span - margin + 1)))
    block = lax.dynamic_slice_in_dim(padded, tile * span, width + 2, axis=1)
    centre = block[1:-1, 1:-1]
    north = 0.5 * (centre + block[2:, 1:-1])
    south = 0.5 * (centre + block[:-2, 1:-1])
    east = 0.5 * (centre + block[1:-1, 2:])
    west = 0.5 * (centre + block[1:-1, :-2])
    diagonal = north + south + east + west + (courant_rows + courant_cols)
    return (north, south, east, west, diagonal)


def column_tiles(field, tiles, width, margin):
    rows, cols = field.shape
    span = cols // tiles
    padded = jnp.pad(field, ((0, 0), (margin, 2 * span - margin)))
    main = padded[:, :cols].reshape(rows, tiles, span)
    extra = padded[:, span : cols + span].reshape(rows, tiles, span)[:, :, : width - span]
    return jnp.concatenate([main, extra], axis=2).transpose(1, 0, 2)


def solve_kernel(spec_ref, north_ref, south_ref, east_ref, west_ref, diag_a_ref, diag_b_ref,
                 inva_ref, invb_ref, invi_ref, imag_ref, out_ref):
    rows, lanes = north_ref.shape

    def coupled(x):
        above = pltpu.roll(x, rows - 1, 0)
        below = pltpu.roll(x, 1, 0)
        after = pltpu.roll(x, lanes - 1, 1)
        before = pltpu.roll(x, 1, 1)
        return (north_ref[...] * above + south_ref[...] * below
                + east_ref[...] * after + west_ref[...] * before)

    first = True
    for sweep in range(SWEEPS):
        for weight in step_weights(DEGREE):
            if first:
                res_real = spec_ref[0]
                res_imag = spec_ref[1]
            else:
                state_real = out_ref[0]
                state_imag = out_ref[1]
                image_real = (diag_a_ref[...] * state_real - imag_ref[...] * state_imag
                              - coupled(state_real))
                image_imag = (diag_b_ref[...] * state_imag + imag_ref[...] * state_real
                              - coupled(state_imag))
                res_real = spec_ref[0] - image_real
                res_imag = spec_ref[1] - image_imag
            corr_real = inva_ref[...] * res_real - invi_ref[...] * res_imag
            corr_imag = invb_ref[...] * res_imag + invi_ref[...] * res_real
            if first:
                out_ref[0] = weight * corr_real
                out_ref[1] = weight * corr_imag
                first = False
            else:
                out_ref[0] = out_ref[0] + weight * corr_real
                out_ref[1] = out_ref[1] + weight * corr_imag


def solve_slots(spectrum, faces, shifts, inside):
    north, south, east, west, diagonal = faces
    real_a, real_b, imag = shifts
    diag_a = real_a + diagonal
    diag_b = real_b + diagonal
    mag_a = diag_a * diag_a + imag * imag
    mag_b = diag_b * diag_b + imag * imag
    inv_a = jnp.where(inside, diag_a / mag_a, 0.0)
    inv_b = jnp.where(inside, diag_b / mag_b, 0.0)
    inv_imag = jnp.where(inside, -imag / mag_a, 0.0)
    operands = (spectrum, north, south + courant_rows, east, west + courant_cols,
                diag_a, diag_b, inv_a, inv_b, inv_imag, jnp.asarray(imag))
    return pl.pallas_call(
        solve_kernel,
        out_shape=jax.ShapeDtypeStruct(spectrum.shape, spectrum.dtype),
    )(*operands)


def body(right_side, kappa):
    steps_dev, rows, cols = right_side.shape
    tiles = lax.axis_size("tm")
    total = steps_dev * tiles
    half = total // 2
    margin = HALO
    span = cols // tiles
    width = span + 2 * margin
    tile = lax.axis_index("tm")
    highest = lax.Precision.HIGHEST
    forward, inverse = transform_matrices(total)

    wide_side, kappa_rows, inside_rows = with_halo(right_side, kappa, margin)
    extended = rows + 2 * margin
    lane = 128
    sent = column_tiles(wide_side, tiles, width, margin).reshape(tiles, -1, lane)
    gathered = gather_steps(sent).reshape(tiles, extended * width)
    spectrum = jnp.dot(forward, gathered, precision=highest)
    spectrum = spectrum.reshape(2, half, extended, width).transpose(0, 2, 1, 3)
    spectrum = spectrum.reshape(2, extended, half * width)

    place = tile * span - margin + jnp.arange(width)
    inside_cols = (place >= 0) & (place < cols)
    inside = inside_rows[:, None] & inside_cols[None, :]
    inside = jnp.tile(inside, (1, half))
    faces = tuple(jnp.tile(f, (1, half)) for f in tile_faces(kappa_rows, tile, tiles, width, margin))
    shifts = slot_shifts(half, total, width)
    solved = solve_slots(spectrum, faces, shifts, inside)

    solved = solved.reshape(2, extended, half, width)[:, margin : margin + rows, :, margin : margin + span]
    solved = solved.transpose(0, 2, 1, 3).reshape(total, rows * span)
    signal = jnp.dot(inverse, solved, precision=highest)
    signal = signal.reshape(total, -1, lane)
    returned = scatter_steps(signal)
    returned = returned.reshape(tiles, rows, span).transpose(1, 0, 2)
    return returned.reshape(steps_dev, rows, cols)


def solution(mesh):
    placed = (P("tm", "row", None), P("row", None))
    return jax.shard_map(
        body, mesh=mesh, in_specs=placed, out_specs=P("tm", "row", None), check_vma=False
    )
```

```python
import functools
import math

import jax
import jax.numpy as jnp
import numpy as np
from jax import lax
from jax.experimental import pallas as pl
from jax.experimental.pallas import tpu as pltpu
from jax.sharding import PartitionSpec as P

SWEEPS = 2
DEGREE = 4
HALO = 8


circulant_alpha = 0.05
courant_rows = 0.5
courant_cols = 0.25
cheb_centre = 1.0
cheb_half = 0.7


def step_weights(count):
    return [
        1.0 / (cheb_centre + cheb_half * math.cos(math.pi * (2 * number + 1) / (2 * count)))
        for number in range(count)
    ]


def with_halo(right_side, kappa, width):
    rows = kappa.shape[0]
    count = lax.axis_size("row")
    forward = [(i, i + 1) for i in range(count - 1)]
    backward = [(target, source) for source, target in forward]
    bottom = jnp.stack([right_side[0, rows - width :], kappa[rows - width :]])
    top = jnp.stack([right_side[0, :width], kappa[:width]])
    bottom, top = lax.optimization_barrier((bottom, top))
    low = lax.ppermute(bottom, "row", forward)
    high = lax.ppermute(top, "row", backward)
    joined = jnp.concatenate([right_side, kappa[None]], axis=0)
    joined = jnp.concatenate([low, joined, high], axis=1)
    place = lax.axis_index("row") * rows - width + jnp.arange(rows + 2 * width)
    inside = (place >= 0) & (place < rows * count)
    return joined[0], joined[1], inside


def transform_matrices(total):
    half = total // 2
    steps = np.arange(total)
    scale = circulant_alpha ** (steps / total)
    forward = np.zeros((total, total))
    inverse = np.zeros((total, total))
    forward[0] = 1.0
    forward[half] = (-1.0) ** steps
    inverse[:, 0] = 1.0
    inverse[:, half] = (-1.0) ** steps
    for slot in range(1, half):
        angle = 2.0 * np.pi * slot * steps / total
        forward[slot] = np.cos(angle)
        forward[half + slot] = -np.sin(angle)
        inverse[:, slot] = 2.0 * np.cos(angle)
        inverse[:, half + slot] = -2.0 * np.sin(angle)
    forward = forward * scale[None, :]
    inverse = inverse / total / scale[:, None]
    return forward.astype(np.float32), inverse.astype(np.float32)


def slot_shifts(half, total, width):
    decay = circulant_alpha ** (1.0 / total)
    slots = np.arange(half)
    theta = 2.0 * np.pi / total * slots
    real_a = 1.0 - decay * np.cos(theta)
    real_b = real_a.copy()
    imag = decay * np.sin(theta)
    real_b[0] = 1.0 + decay
    imag[0] = 0.0
    spread = lambda v: np.repeat(v.astype(np.float32), width)[None, :]
    return spread(real_a), spread(real_b), spread(imag)


def tile_faces(kappa_rows, tile, tiles, width, margin):
    rows, cols = kappa_rows.shape
    span = cols // tiles
    padded = jnp.pad(kappa_rows, ((1, 1), (margin + 1, width - span - margin + 1)))
    block = lax.dynamic_slice_in_dim(padded, tile * span, width + 2, axis=1)
    centre = block[1:-1, 1:-1]
    north = 0.5 * (centre + block[2:, 1:-1])
    south = 0.5 * (centre + block[:-2, 1:-1])
    east = 0.5 * (centre + block[1:-1, 2:])
    west = 0.5 * (centre + block[1:-1, :-2])
    diagonal = north + south + east + west + (courant_rows + courant_cols)
    return (north, south, east, west, diagonal)


def column_tiles(field, tiles, width, margin):
    rows, cols = field.shape
    span = cols // tiles
    padded = jnp.pad(field, ((0, 0), (margin, 2 * span - margin)))
    main = padded[:, :cols].reshape(rows, tiles, span)
    extra = padded[:, span : cols + span].reshape(rows, tiles, span)[:, :, : width - span]
    return jnp.concatenate([main, extra], axis=2).transpose(1, 0, 2)


def solve_kernel(margin, spec_ref, north_ref, south_ref, east_ref, west_ref, diag_a_ref, diag_b_ref,
                 inva_ref, invb_ref, invi_ref, imag_ref, interior_ref, out_ref):
    rows, lanes = north_ref.shape

    def coupled(x):
        above = pltpu.roll(x, rows - 1, 0)
        below = pltpu.roll(x, 1, 0)
        after = pltpu.roll(x, lanes - 1, 1)
        before = pltpu.roll(x, 1, 1)
        return (north_ref[...] * above + south_ref[...] * below
                + east_ref[...] * after + west_ref[...] * before)

    first = True
    for sweep in range(SWEEPS):
        for weight in step_weights(DEGREE):
            if first:
                res_real = spec_ref[0]
                res_imag = spec_ref[1]
            else:
                state_real = out_ref[0]
                state_imag = out_ref[1]
                image_real = (diag_a_ref[...] * state_real - imag_ref[...] * state_imag
                              - coupled(state_real))
                image_imag = (diag_b_ref[...] * state_imag + imag_ref[...] * state_real
                              - coupled(state_imag))
                res_real = spec_ref[0] - image_real
                res_imag = spec_ref[1] - image_imag
            corr_real = inva_ref[...] * res_real - invi_ref[...] * res_imag
            corr_imag = invb_ref[...] * res_imag + invi_ref[...] * res_real
            if first:
                out_ref[0] = weight * corr_real
                out_ref[1] = weight * corr_imag
                first = False
            else:
                out_ref[0] = out_ref[0] + weight * corr_real
                out_ref[1] = out_ref[1] + weight * corr_imag
    inner = interior_ref.shape[1]
    interior_ref[...] = out_ref[:, margin : margin + inner]


def solve_slots(spectrum, faces, shifts, inside, margin):
    north, south, east, west, diagonal = faces
    real_a, real_b, imag = shifts
    diag_a = real_a + diagonal
    diag_b = real_b + diagonal
    mag_a = diag_a * diag_a + imag * imag
    mag_b = diag_b * diag_b + imag * imag
    inv_a = jnp.where(inside, diag_a / mag_a, 0.0)
    inv_b = jnp.where(inside, diag_b / mag_b, 0.0)
    inv_imag = jnp.where(inside, -imag / mag_a, 0.0)
    operands = (spectrum, north, south + courant_rows, east, west + courant_cols,
                diag_a, diag_b, inv_a, inv_b, inv_imag, jnp.asarray(imag))
    parts, extended, lanes = spectrum.shape
    return pl.pallas_call(
        functools.partial(solve_kernel, margin),
        out_shape=jax.ShapeDtypeStruct((parts, extended - 2 * margin, lanes), spectrum.dtype),
        scratch_shapes=[pltpu.VMEM(spectrum.shape, jnp.float32)],
    )(*operands)


def body(right_side, kappa):
    steps_dev, rows, cols = right_side.shape
    tiles = lax.axis_size("tm")
    total = steps_dev * tiles
    half = total // 2
    margin = HALO
    span = cols // tiles
    width = span + 2 * margin
    tile = lax.axis_index("tm")
    highest = lax.Precision.HIGHEST
    forward, inverse = transform_matrices(total)

    wide_side, kappa_rows, inside_rows = with_halo(right_side, kappa, margin)
    extended = rows + 2 * margin
    lane = 128
    sent = column_tiles(wide_side, tiles, width, margin).reshape(tiles, -1, lane)
    gathered = lax.all_to_all(sent, "tm", 0, 0, tiled=True).reshape(tiles, extended * width)
    spectrum = jnp.dot(forward, gathered, precision=highest)
    spectrum = spectrum.reshape(2, half, extended, width).transpose(0, 2, 1, 3)
    spectrum = spectrum.reshape(2, extended, half * width)

    place = tile * span - margin + jnp.arange(width)
    inside_cols = (place >= 0) & (place < cols)
    inside = inside_rows[:, None] & inside_cols[None, :]
    inside = jnp.tile(inside, (1, half))
    faces = tuple(jnp.tile(f, (1, half)) for f in tile_faces(kappa_rows, tile, tiles, width, margin))
    shifts = slot_shifts(half, total, width)
    solved = solve_slots(spectrum, faces, shifts, inside, margin)

    solved = solved.reshape(2, rows, half, width)[..., margin : margin + span]
    solved = solved.transpose(0, 2, 1, 3).reshape(total, rows * span)
    signal = jnp.dot(inverse, solved, precision=highest)
    signal = signal.reshape(total, -1, lane)
    returned = lax.all_to_all(signal, "tm", 0, 0, tiled=True)
    returned = returned.reshape(tiles, rows, span).transpose(1, 0, 2)
    return returned.reshape(steps_dev, rows, cols)


def solution(mesh):
    placed = (P("tm", "row", None), P("row", None))
    return jax.shard_map(
        body, mesh=mesh, in_specs=placed, out_specs=P("tm", "row", None), check_vma=False
    )
```

```python
import math

import jax
import jax.numpy as jnp
import numpy as np
from jax import lax
from jax.experimental import pallas as pl
from jax.experimental.pallas import tpu as pltpu
from jax.sharding import PartitionSpec as P

SWEEPS = 2
DEGREE = 4
HALO = 8


circulant_alpha = 0.05
courant_rows = 0.5
courant_cols = 0.25
cheb_centre = 1.0
cheb_half = 0.7


def step_weights(count):
    return [
        1.0 / (cheb_centre + cheb_half * math.cos(math.pi * (2 * number + 1) / (2 * count)))
        for number in range(count)
    ]


def with_halo(right_side, kappa, width):
    rows = kappa.shape[0]
    count = lax.axis_size("row")
    forward = [(i, i + 1) for i in range(count - 1)]
    backward = [(target, source) for source, target in forward]
    bottom = jnp.stack([right_side[0, rows - width :], kappa[rows - width :]])
    top = jnp.stack([right_side[0, :width], kappa[:width]])
    bottom, top = lax.optimization_barrier((bottom, top))
    low = lax.ppermute(bottom, "row", forward)
    high = lax.ppermute(top, "row", backward)
    wide_side = jnp.concatenate([low[0], right_side[0], high[0]], axis=0)
    kappa_rows = jnp.concatenate([low[1], kappa, high[1]], axis=0)
    place = lax.axis_index("row") * rows - width + jnp.arange(rows + 2 * width)
    inside = (place >= 0) & (place < rows * count)
    return wide_side, kappa_rows, inside


def transform_matrices(total):
    half = total // 2
    steps = np.arange(total)
    scale = circulant_alpha ** (steps / total)
    forward = np.zeros((total, total))
    inverse = np.zeros((total, total))
    forward[0] = 1.0
    forward[half] = (-1.0) ** steps
    inverse[:, 0] = 1.0
    inverse[:, half] = (-1.0) ** steps
    for slot in range(1, half):
        angle = 2.0 * np.pi * slot * steps / total
        forward[slot] = np.cos(angle)
        forward[half + slot] = -np.sin(angle)
        inverse[:, slot] = 2.0 * np.cos(angle)
        inverse[:, half + slot] = -2.0 * np.sin(angle)
    forward = forward * scale[None, :]
    inverse = inverse / total / scale[:, None]
    return forward.astype(np.float32), inverse.astype(np.float32)


def slot_shifts(half, total, width):
    decay = circulant_alpha ** (1.0 / total)
    slots = np.arange(half)
    theta = 2.0 * np.pi / total * slots
    real_a = 1.0 - decay * np.cos(theta)
    real_b = real_a.copy()
    imag = decay * np.sin(theta)
    real_b[0] = 1.0 + decay
    imag[0] = 0.0
    spread = lambda v: np.repeat(v.astype(np.float32), width)[None, :]
    return spread(real_a), spread(real_b), spread(imag)


def tile_faces(kappa_rows, tile, tiles, width, margin):
    rows, cols = kappa_rows.shape
    span = cols // tiles
    padded = jnp.pad(kappa_rows, ((1, 1), (margin + 1, width - span - margin + 1)))
    block = lax.dynamic_slice_in_dim(padded, tile * span, width + 2, axis=1)
    centre = block[1:-1, 1:-1]
    north = 0.5 * (centre + block[2:, 1:-1])
    south = 0.5 * (centre + block[:-2, 1:-1])
    east = 0.5 * (centre + block[1:-1, 2:])
    west = 0.5 * (centre + block[1:-1, :-2])
    diagonal = north + south + east + west + (courant_rows + courant_cols)
    return (north, south, east, west, diagonal)


def column_tiles(field, tiles, width, margin):
    rows, cols = field.shape
    span = cols // tiles
    padded = jnp.pad(field, ((0, 0), (margin, 2 * span - margin)))
    main = padded[:, :cols].reshape(rows, tiles, span)
    extra = padded[:, span : cols + span].reshape(rows, tiles, span)[:, :, : width - span]
    return jnp.concatenate([main, extra], axis=2).transpose(1, 0, 2)


def solve_kernel(spec_ref, north_ref, south_ref, east_ref, west_ref, diag_a_ref, diag_b_ref,
                 inva_ref, invb_ref, invi_ref, imag_ref, out_ref):
    rows, lanes = north_ref.shape

    def coupled(x):
        above = pltpu.roll(x, rows - 1, 0)
        below = pltpu.roll(x, 1, 0)
        after = pltpu.roll(x, lanes - 1, 1)
        before = pltpu.roll(x, 1, 1)
        return (north_ref[...] * above + south_ref[...] * below
                + east_ref[...] * after + west_ref[...] * before)

    first = True
    for sweep in range(SWEEPS):
        for weight in step_weights(DEGREE):
            if first:
                res_real = spec_ref[0]
                res_imag = spec_ref[1]
            else:
                state_real = out_ref[0]
                state_imag = out_ref[1]
                image_real = (diag_a_ref[...] * state_real - imag_ref[...] * state_imag
                              - coupled(state_real))
                image_imag = (diag_b_ref[...] * state_imag + imag_ref[...] * state_real
                              - coupled(state_imag))
                res_real = spec_ref[0] - image_real
                res_imag = spec_ref[1] - image_imag
            corr_real = inva_ref[...] * res_real - invi_ref[...] * res_imag
            corr_imag = invb_ref[...] * res_imag + invi_ref[...] * res_real
            if first:
                out_ref[0] = weight * corr_real
                out_ref[1] = weight * corr_imag
                first = False
            else:
                out_ref[0] = out_ref[0] + weight * corr_real
                out_ref[1] = out_ref[1] + weight * corr_imag


def solve_slots(spectrum, faces, shifts, inside):
    north, south, east, west, diagonal = faces
    real_a, real_b, imag = shifts
    diag_a = real_a + diagonal
    diag_b = real_b + diagonal
    mag_a = diag_a * diag_a + imag * imag
    mag_b = diag_b * diag_b + imag * imag
    inv_a = jnp.where(inside, diag_a / mag_a, 0.0)
    inv_b = jnp.where(inside, diag_b / mag_b, 0.0)
    inv_imag = jnp.where(inside, -imag / mag_a, 0.0)
    operands = (spectrum, north, south + courant_rows, east, west + courant_cols,
                diag_a, diag_b, inv_a, inv_b, inv_imag, jnp.asarray(imag))
    return pl.pallas_call(
        solve_kernel,
        out_shape=jax.ShapeDtypeStruct(spectrum.shape, spectrum.dtype),
    )(*operands)


def body(right_side, kappa):
    steps_dev, rows, cols = right_side.shape
    tiles = lax.axis_size("tm")
    total = steps_dev * tiles
    half = total // 2
    margin = HALO
    span = cols // tiles
    width = span + 2 * margin
    tile = lax.axis_index("tm")
    highest = lax.Precision.HIGHEST
    forward, inverse = transform_matrices(total)

    wide_side, kappa_rows, inside_rows = with_halo(right_side, kappa, margin)
    extended = rows + 2 * margin
    lane = 128
    sent = column_tiles(wide_side, tiles, width, margin).reshape(tiles, -1, lane)
    gathered = lax.all_to_all(sent, "tm", 0, 0, tiled=True).reshape(tiles, extended * width)
    spectrum = jnp.dot(forward, gathered, precision=highest)
    spectrum = spectrum.reshape(2, half, extended, width).transpose(0, 2, 1, 3)
    spectrum = spectrum.reshape(2, extended, half * width)

    place = tile * span - margin + jnp.arange(width)
    inside_cols = (place >= 0) & (place < cols)
    inside = inside_rows[:, None] & inside_cols[None, :]
    inside = jnp.tile(inside, (1, half))
    faces = tuple(jnp.tile(f, (1, half)) for f in tile_faces(kappa_rows, tile, tiles, width, margin))
    shifts = slot_shifts(half, total, width)
    solved = solve_slots(spectrum, faces, shifts, inside)

    solved = solved.reshape(2, extended, half, width)[:, margin : margin + rows, :, margin : margin + span]
    solved = solved.transpose(0, 2, 1, 3).reshape(total, rows * span)
    signal = jnp.dot(inverse, solved, precision=highest)
    signal = signal.reshape(total, -1, lane)
    returned = lax.all_to_all(signal, "tm", 0, 0, tiled=True)
    returned = returned.reshape(tiles, rows, span).transpose(1, 0, 2)
    return returned.reshape(steps_dev, rows, cols)


def solution(mesh):
    placed = (P("tm", "row", None), P("row", None))
    return jax.shard_map(
        body, mesh=mesh, in_specs=placed, out_specs=P("tm", "row", None), check_vma=False
    )
```

```python
import math

import jax
import jax.numpy as jnp
import numpy as np
from jax import lax
from jax.experimental import pallas as pl
from jax.experimental.pallas import tpu as pltpu
from jax.sharding import PartitionSpec as P

SWEEPS = 2
DEGREE = 4
HALO = 8


circulant_alpha = 0.05
courant_rows = 0.5
courant_cols = 0.25
cheb_centre = 1.0
cheb_half = 0.7


def step_weights(count):
    return [
        1.0 / (cheb_centre + cheb_half * math.cos(math.pi * (2 * number + 1) / (2 * count)))
        for number in range(count)
    ]


def with_halo(right_side, kappa, width):
    rows = kappa.shape[0]
    count = lax.axis_size("row")
    forward = [(i, i + 1) for i in range(count - 1)]
    backward = [(target, source) for source, target in forward]
    bottom = jnp.stack([right_side[0, rows - width :], kappa[rows - width :]])
    top = jnp.stack([right_side[0, :width], kappa[:width]])
    bottom, top = lax.optimization_barrier((bottom, top))
    low = lax.ppermute(bottom, "row", forward)
    high = lax.ppermute(top, "row", backward)
    wide_side = jnp.concatenate([low[0], right_side[0], high[0]], axis=0)
    kappa_rows = jnp.concatenate([low[1], kappa, high[1]], axis=0)
    place = lax.axis_index("row") * rows - width + jnp.arange(rows + 2 * width)
    inside = (place >= 0) & (place < rows * count)
    return wide_side, kappa_rows, inside


def transform_matrices(total):
    half = total // 2
    steps = np.arange(total)
    scale = circulant_alpha ** (steps / total)
    forward = np.zeros((total, total))
    inverse = np.zeros((total, total))
    forward[0] = 1.0
    forward[half] = (-1.0) ** steps
    inverse[:, 0] = 1.0
    inverse[:, half] = (-1.0) ** steps
    for slot in range(1, half):
        angle = 2.0 * np.pi * slot * steps / total
        forward[slot] = np.cos(angle)
        forward[half + slot] = -np.sin(angle)
        inverse[:, slot] = 2.0 * np.cos(angle)
        inverse[:, half + slot] = -2.0 * np.sin(angle)
    forward = forward * scale[None, :]
    inverse = inverse / total / scale[:, None]
    return forward.astype(np.float32), inverse.astype(np.float32)


def slot_shifts(half, total, width):
    decay = circulant_alpha ** (1.0 / total)
    slots = np.arange(half)
    theta = 2.0 * np.pi / total * slots
    real_a = 1.0 - decay * np.cos(theta)
    real_b = real_a.copy()
    imag = decay * np.sin(theta)
    real_b[0] = 1.0 + decay
    imag[0] = 0.0
    spread = lambda v: np.repeat(v.astype(np.float32), width)[None, :]
    return spread(real_a), spread(real_b), spread(imag)


def tile_faces(kappa_rows, tile, tiles, width, margin):
    rows, cols = kappa_rows.shape
    span = cols // tiles
    padded = jnp.pad(kappa_rows, ((1, 1), (margin + 1, width - span - margin + 1)))
    block = lax.dynamic_slice_in_dim(padded, tile * span, width + 2, axis=1)
    centre = block[1:-1, 1:-1]
    north = 0.5 * (centre + block[2:, 1:-1])
    south = 0.5 * (centre + block[:-2, 1:-1])
    east = 0.5 * (centre + block[1:-1, 2:])
    west = 0.5 * (centre + block[1:-1, :-2])
    diagonal = north + south + east + west + (courant_rows + courant_cols)
    return (north, south, east, west, diagonal)


def column_tiles(field, tiles, width, margin):
    rows, cols = field.shape
    span = cols // tiles
    padded = jnp.pad(field, ((0, 0), (margin, 2 * span - margin)))
    main = padded[:, :cols].reshape(rows, tiles, span)
    extra = padded[:, span : cols + span].reshape(rows, tiles, span)[:, :, : width - span]
    return jnp.concatenate([main, extra], axis=2).transpose(1, 0, 2)


def solve_kernel(spec_ref, north_ref, south_ref, east_ref, west_ref, diag_a_ref, diag_b_ref,
                 inva_ref, invb_ref, invi_ref, imag_ref, out_ref):
    rows, lanes = north_ref.shape

    def coupled(x):
        above = pltpu.roll(x, rows - 1, 0)
        below = pltpu.roll(x, 1, 0)
        after = pltpu.roll(x, lanes - 1, 1)
        before = pltpu.roll(x, 1, 1)
        return (north_ref[...] * above + south_ref[...] * below
                + east_ref[...] * after + west_ref[...] * before)

    first = True
    for sweep in range(SWEEPS):
        for weight in step_weights(DEGREE):
            if first:
                res_real = spec_ref[0]
                res_imag = spec_ref[1]
            else:
                state_real = out_ref[0]
                state_imag = out_ref[1]
                image_real = (diag_a_ref[...] * state_real - imag_ref[...] * state_imag
                              - coupled(state_real))
                image_imag = (diag_b_ref[...] * state_imag + imag_ref[...] * state_real
                              - coupled(state_imag))
                res_real = spec_ref[0] - image_real
                res_imag = spec_ref[1] - image_imag
            corr_real = inva_ref[...] * res_real - invi_ref[...] * res_imag
            corr_imag = invb_ref[...] * res_imag + invi_ref[...] * res_real
            if first:
                out_ref[0] = weight * corr_real
                out_ref[1] = weight * corr_imag
                first = False
            else:
                out_ref[0] = out_ref[0] + weight * corr_real
                out_ref[1] = out_ref[1] + weight * corr_imag


def solve_slots(spectrum, faces, shifts, inside):
    north, south, east, west, diagonal = faces
    real_a, real_b, imag = shifts
    diag_a = real_a + diagonal
    diag_b = real_b + diagonal
    mag_a = diag_a * diag_a + imag * imag
    mag_b = diag_b * diag_b + imag * imag
    inv_a = jnp.where(inside, diag_a / mag_a, 0.0)
    inv_b = jnp.where(inside, diag_b / mag_b, 0.0)
    inv_imag = jnp.where(inside, -imag / mag_a, 0.0)
    operands = (spectrum, north, south + courant_rows, east, west + courant_cols,
                diag_a, diag_b, inv_a, inv_b, inv_imag, jnp.asarray(imag))
    return pl.pallas_call(
        solve_kernel,
        out_shape=jax.ShapeDtypeStruct(spectrum.shape, spectrum.dtype),
    )(*operands)


def body(right_side, kappa):
    steps_dev, rows, cols = right_side.shape
    tiles = lax.axis_size("tm")
    total = steps_dev * tiles
    half = total // 2
    margin = HALO
    span = cols // tiles
    width = span + 2 * margin
    tile = lax.axis_index("tm")
    highest = lax.Precision.HIGH
    forward, inverse = transform_matrices(total)

    wide_side, kappa_rows, inside_rows = with_halo(right_side, kappa, margin)
    extended = rows + 2 * margin
    lane = 128
    sent = column_tiles(wide_side, tiles, width, margin).reshape(tiles, -1, lane)
    gathered = lax.all_to_all(sent, "tm", 0, 0, tiled=True).reshape(tiles, extended * width)
    spectrum = jnp.dot(forward, gathered, precision=highest)
    spectrum = spectrum.reshape(2, half, extended, width).transpose(0, 2, 1, 3)
    spectrum = spectrum.reshape(2, extended, half * width)

    place = tile * span - margin + jnp.arange(width)
    inside_cols = (place >= 0) & (place < cols)
    inside = inside_rows[:, None] & inside_cols[None, :]
    inside = jnp.tile(inside, (1, half))
    faces = tuple(jnp.tile(f, (1, half)) for f in tile_faces(kappa_rows, tile, tiles, width, margin))
    shifts = slot_shifts(half, total, width)
    solved = solve_slots(spectrum, faces, shifts, inside)

    solved = solved.reshape(2, extended, half, width)[:, margin : margin + rows, :, margin : margin + span]
    solved = solved.transpose(0, 2, 1, 3).reshape(total, rows * span)
    signal = jnp.dot(inverse, solved, precision=highest)
    signal = signal.reshape(total, -1, lane)
    returned = lax.all_to_all(signal, "tm", 0, 0, tiled=True)
    returned = returned.reshape(tiles, rows, span).transpose(1, 0, 2)
    return returned.reshape(steps_dev, rows, cols)


def solution(mesh):
    placed = (P("tm", "row", None), P("row", None))
    return jax.shard_map(
        body, mesh=mesh, in_specs=placed, out_specs=P("tm", "row", None), check_vma=False
    )
```

```python
import math

import jax
import jax.numpy as jnp
import numpy as np
from jax import lax
from jax.experimental import pallas as pl
from jax.experimental.pallas import tpu as pltpu
from jax.sharding import PartitionSpec as P

SWEEPS = 2
DEGREE = 4
HALO = 8


circulant_alpha = 0.05
courant_rows = 0.5
courant_cols = 0.25
cheb_centre = 1.0
cheb_half = 0.7


def step_weights(count):
    return [
        1.0 / (cheb_centre + cheb_half * math.cos(math.pi * (2 * number + 1) / (2 * count)))
        for number in range(count)
    ]


def with_halo(right_side, kappa, width):
    rows = kappa.shape[0]
    count = lax.axis_size("row")
    forward = [(i, i + 1) for i in range(count - 1)]
    backward = [(target, source) for source, target in forward]
    bottom = jnp.stack([right_side[0, rows - width :], kappa[rows - width :]])
    top = jnp.stack([right_side[0, :width], kappa[:width]])
    bottom, top = lax.optimization_barrier((bottom, top))
    low = lax.ppermute(bottom, "row", forward)
    high = lax.ppermute(top, "row", backward)
    wide_side = jnp.concatenate([low[0], right_side[0], high[0]], axis=0)
    kappa_rows = jnp.concatenate([low[1], kappa, high[1]], axis=0)
    place = lax.axis_index("row") * rows - width + jnp.arange(rows + 2 * width)
    inside = (place >= 0) & (place < rows * count)
    return wide_side, kappa_rows, inside


def transform_matrices(total):
    half = total // 2
    steps = np.arange(total)
    scale = circulant_alpha ** (steps / total)
    forward = np.zeros((total, total))
    inverse = np.zeros((total, total))
    forward[0] = 1.0
    forward[half] = (-1.0) ** steps
    inverse[:, 0] = 1.0
    inverse[:, half] = (-1.0) ** steps
    for slot in range(1, half):
        angle = 2.0 * np.pi * slot * steps / total
        forward[slot] = np.cos(angle)
        forward[half + slot] = -np.sin(angle)
        inverse[:, slot] = 2.0 * np.cos(angle)
        inverse[:, half + slot] = -2.0 * np.sin(angle)
    forward = forward * scale[None, :]
    inverse = inverse / total / scale[:, None]
    return forward.astype(np.float32), inverse.astype(np.float32)


def slot_shifts(half, total, width):
    decay = circulant_alpha ** (1.0 / total)
    slots = np.arange(half)
    theta = 2.0 * np.pi / total * slots
    real_a = 1.0 - decay * np.cos(theta)
    real_b = real_a.copy()
    imag = decay * np.sin(theta)
    real_b[0] = 1.0 + decay
    imag[0] = 0.0
    spread = lambda v: np.repeat(v.astype(np.float32), width)[None, :]
    return spread(real_a), spread(real_b), spread(imag)


def tile_faces(kappa_rows, tile, tiles, width, margin):
    rows, cols = kappa_rows.shape
    span = cols // tiles
    padded = jnp.pad(kappa_rows, ((1, 1), (margin + 1, width - span - margin + 1)))
    block = lax.dynamic_slice_in_dim(padded, tile * span, width + 2, axis=1)
    centre = block[1:-1, 1:-1]
    north = 0.5 * (centre + block[2:, 1:-1])
    south = 0.5 * (centre + block[:-2, 1:-1])
    east = 0.5 * (centre + block[1:-1, 2:])
    west = 0.5 * (centre + block[1:-1, :-2])
    diagonal = north + south + east + west + (courant_rows + courant_cols)
    return (north, south, east, west, diagonal)


def column_tiles(field, tiles, width, margin):
    rows, cols = field.shape
    span = cols // tiles
    padded = jnp.pad(field, ((0, 0), (margin, 2 * span - margin)))
    main = padded[:, :cols].reshape(rows, tiles, span)
    extra = padded[:, span : cols + span].reshape(rows, tiles, span)[:, :, : width - span]
    return jnp.concatenate([main, extra], axis=2).transpose(1, 0, 2)


def solve_kernel(spec_ref, north_ref, south_ref, east_ref, west_ref, diag_a_ref, diag_b_ref,
                 inva_ref, invb_ref, invi_ref, imag_ref, out_ref):
    rows, lanes = north_ref.shape

    def coupled(x):
        above = pltpu.roll(x, rows - 1, 0)
        below = pltpu.roll(x, 1, 0)
        after = pltpu.roll(x, lanes - 1, 1)
        before = pltpu.roll(x, 1, 1)
        return (north_ref[...] * above + south_ref[...] * below
                + east_ref[...] * after + west_ref[...] * before)

    first = True
    for sweep in range(SWEEPS):
        for weight in step_weights(DEGREE):
            if first:
                res_real = spec_ref[0]
                res_imag = spec_ref[1]
            else:
                state_real = out_ref[0]
                state_imag = out_ref[1]
                image_real = (diag_a_ref[...] * state_real - imag_ref[...] * state_imag
                              - coupled(state_real))
                image_imag = (diag_b_ref[...] * state_imag + imag_ref[...] * state_real
                              - coupled(state_imag))
                res_real = spec_ref[0] - image_real
                res_imag = spec_ref[1] - image_imag
            corr_real = inva_ref[...] * res_real - invi_ref[...] * res_imag
            corr_imag = invb_ref[...] * res_imag + invi_ref[...] * res_real
            if first:
                out_ref[0] = weight * corr_real
                out_ref[1] = weight * corr_imag
                first = False
            else:
                out_ref[0] = out_ref[0] + weight * corr_real
                out_ref[1] = out_ref[1] + weight * corr_imag


def solve_slots(spectrum, faces, shifts, inside):
    north, south, east, west, diagonal = faces
    real_a, real_b, imag = shifts
    diag_a = real_a + diagonal
    diag_b = real_b + diagonal
    mag_a = diag_a * diag_a + imag * imag
    mag_b = diag_b * diag_b + imag * imag
    inv_a = jnp.where(inside, diag_a / mag_a, 0.0)
    inv_b = jnp.where(inside, diag_b / mag_b, 0.0)
    inv_imag = jnp.where(inside, -imag / mag_a, 0.0)
    operands = (spectrum, north, south + courant_rows, east, west + courant_cols,
                diag_a, diag_b, inv_a, inv_b, inv_imag, jnp.asarray(imag))
    parts, extended, lanes = spectrum.shape
    blocks = 2
    block = lanes // blocks
    field = pl.BlockSpec((extended, block), lambda i: (0, i))
    pair = pl.BlockSpec((parts, extended, block), lambda i: (0, 0, i))
    row = pl.BlockSpec((1, block), lambda i: (0, i))
    return pl.pallas_call(
        solve_kernel,
        grid=(blocks,),
        in_specs=[pair] + [field] * 9 + [row],
        out_specs=pair,
        out_shape=jax.ShapeDtypeStruct(spectrum.shape, spectrum.dtype),
    )(*operands)


def body(right_side, kappa):
    steps_dev, rows, cols = right_side.shape
    tiles = lax.axis_size("tm")
    total = steps_dev * tiles
    half = total // 2
    margin = HALO
    span = cols // tiles
    width = span + 2 * margin
    tile = lax.axis_index("tm")
    highest = lax.Precision.HIGHEST
    forward, inverse = transform_matrices(total)

    wide_side, kappa_rows, inside_rows = with_halo(right_side, kappa, margin)
    extended = rows + 2 * margin
    lane = 128
    sent = column_tiles(wide_side, tiles, width, margin).reshape(tiles, -1, lane)
    gathered = lax.all_to_all(sent, "tm", 0, 0, tiled=True).reshape(tiles, extended * width)
    spectrum = jnp.dot(forward, gathered, precision=highest)
    spectrum = spectrum.reshape(2, half, extended, width).transpose(0, 2, 1, 3)
    spectrum = spectrum.reshape(2, extended, half * width)

    place = tile * span - margin + jnp.arange(width)
    inside_cols = (place >= 0) & (place < cols)
    inside = inside_rows[:, None] & inside_cols[None, :]
    inside = jnp.tile(inside, (1, half))
    faces = tuple(jnp.tile(f, (1, half)) for f in tile_faces(kappa_rows, tile, tiles, width, margin))
    shifts = slot_shifts(half, total, width)
    solved = solve_slots(spectrum, faces, shifts, inside)

    solved = solved.reshape(2, extended, half, width)[:, margin : margin + rows, :, margin : margin + span]
    solved = solved.transpose(0, 2, 1, 3).reshape(total, rows * span)
    signal = jnp.dot(inverse, solved, precision=highest)
    signal = signal.reshape(total, -1, lane)
    returned = lax.all_to_all(signal, "tm", 0, 0, tiled=True)
    returned = returned.reshape(tiles, rows, span).transpose(1, 0, 2)
    return returned.reshape(steps_dev, rows, cols)


def solution(mesh):
    placed = (P("tm", "row", None), P("row", None))
    return jax.shard_map(
        body, mesh=mesh, in_specs=placed, out_specs=P("tm", "row", None), check_vma=False
    )
```

```python
import math

import jax
import jax.numpy as jnp
import numpy as np
from jax import lax
from jax.experimental import pallas as pl
from jax.experimental.pallas import tpu as pltpu
from jax.sharding import PartitionSpec as P

SWEEPS = 2
DEGREE = 4
HALO = 8


circulant_alpha = 0.05
courant_rows = 0.5
courant_cols = 0.25
cheb_centre = 1.0
cheb_half = 0.7


def step_weights(count):
    return [
        1.0 / (cheb_centre + cheb_half * math.cos(math.pi * (2 * number + 1) / (2 * count)))
        for number in range(count)
    ]


def with_halo(right_side, kappa, width):
    rows = kappa.shape[0]
    count = lax.axis_size("row")
    forward = [(i, i + 1) for i in range(count - 1)]
    backward = [(target, source) for source, target in forward]
    bottom = jnp.stack([right_side[0, rows - width :], kappa[rows - width :]])
    top = jnp.stack([right_side[0, :width], kappa[:width]])
    bottom, top = lax.optimization_barrier((bottom, top))
    low = lax.ppermute(bottom, "row", forward)
    high = lax.ppermute(top, "row", backward)
    wide_side = jnp.concatenate([low[0], right_side[0], high[0]], axis=0)
    kappa_rows = jnp.concatenate([low[1], kappa, high[1]], axis=0)
    place = lax.axis_index("row") * rows - width + jnp.arange(rows + 2 * width)
    inside = (place >= 0) & (place < rows * count)
    return wide_side, kappa_rows, inside


def transform_matrices(total):
    half = total // 2
    steps = np.arange(total)
    scale = circulant_alpha ** (steps / total)
    forward = np.zeros((total, total))
    inverse = np.zeros((total, total))
    forward[0] = 1.0
    forward[half] = (-1.0) ** steps
    inverse[:, 0] = 1.0
    inverse[:, half] = (-1.0) ** steps
    for slot in range(1, half):
        angle = 2.0 * np.pi * slot * steps / total
        forward[slot] = np.cos(angle)
        forward[half + slot] = -np.sin(angle)
        inverse[:, slot] = 2.0 * np.cos(angle)
        inverse[:, half + slot] = -2.0 * np.sin(angle)
    forward = forward * scale[None, :]
    inverse = inverse / total / scale[:, None]
    return forward.astype(np.float32), inverse.astype(np.float32)


def slot_shifts(half, total, width):
    decay = circulant_alpha ** (1.0 / total)
    slots = np.arange(half)
    theta = 2.0 * np.pi / total * slots
    real_a = 1.0 - decay * np.cos(theta)
    real_b = real_a.copy()
    imag = decay * np.sin(theta)
    real_b[0] = 1.0 + decay
    imag[0] = 0.0
    spread = lambda v: np.repeat(v.astype(np.float32), width)[None, :]
    return spread(real_a), spread(real_b), spread(imag)


def tile_faces(kappa_rows, tile, tiles, width, margin):
    rows, cols = kappa_rows.shape
    span = cols // tiles
    padded = jnp.pad(kappa_rows, ((1, 1), (margin + 1, width - span - margin + 1)))
    block = lax.dynamic_slice_in_dim(padded, tile * span, width + 2, axis=1)
    centre = block[1:-1, 1:-1]
    north = 0.5 * (centre + block[2:, 1:-1])
    south = 0.5 * (centre + block[:-2, 1:-1])
    east = 0.5 * (centre + block[1:-1, 2:])
    west = 0.5 * (centre + block[1:-1, :-2])
    diagonal = north + south + east + west + (courant_rows + courant_cols)
    return (north, south, east, west, diagonal)


def column_tiles(field, tiles, width, margin):
    rows, cols = field.shape
    span = cols // tiles
    padded = jnp.pad(field, ((0, 0), (margin, 2 * span - margin)))
    main = padded[:, :cols].reshape(rows, tiles, span)
    extra = padded[:, span : cols + span].reshape(rows, tiles, span)[:, :, : width - span]
    return jnp.concatenate([main, extra], axis=2).transpose(1, 0, 2)


def solve_kernel(spec_ref, north_ref, south_ref, east_ref, west_ref, diag_a_ref, diag_b_ref,
                 inva_ref, invb_ref, invi_ref, imag_ref, out_ref):
    rows, lanes = north_ref.shape

    def coupled(x):
        above = pltpu.roll(x, rows - 1, 0)
        below = pltpu.roll(x, 1, 0)
        after = pltpu.roll(x, lanes - 1, 1)
        before = pltpu.roll(x, 1, 1)
        return (north_ref[...] * above + south_ref[...] * below
                + east_ref[...] * after + west_ref[...] * before)

    first = True
    for sweep in range(SWEEPS):
        for weight in step_weights(DEGREE):
            if first:
                res_real = spec_ref[0]
                res_imag = spec_ref[1]
            else:
                state_real = out_ref[0]
                state_imag = out_ref[1]
                image_real = (diag_a_ref[...] * state_real - imag_ref[...] * state_imag
                              - coupled(state_real))
                image_imag = (diag_b_ref[...] * state_imag + imag_ref[...] * state_real
                              - coupled(state_imag))
                res_real = spec_ref[0] - image_real
                res_imag = spec_ref[1] - image_imag
            corr_real = inva_ref[...] * res_real - invi_ref[...] * res_imag
            corr_imag = invb_ref[...] * res_imag + invi_ref[...] * res_real
            if first:
                out_ref[0] = weight * corr_real
                out_ref[1] = weight * corr_imag
                first = False
            else:
                out_ref[0] = out_ref[0] + weight * corr_real
                out_ref[1] = out_ref[1] + weight * corr_imag


def solve_slots(spectrum, faces, shifts, inside):
    north, south, east, west, diagonal = faces
    real_a, real_b, imag = shifts
    diag_a = real_a + diagonal
    diag_b = real_b + diagonal
    mag_a = diag_a * diag_a + imag * imag
    mag_b = diag_b * diag_b + imag * imag
    inv_a = jnp.where(inside, diag_a / mag_a, 0.0)
    inv_b = jnp.where(inside, diag_b / mag_b, 0.0)
    inv_imag = jnp.where(inside, -imag / mag_a, 0.0)
    operands = (spectrum, north, south + courant_rows, east, west + courant_cols,
                diag_a, diag_b, inv_a, inv_b, inv_imag, jnp.asarray(imag))
    return pl.pallas_call(
        solve_kernel,
        out_shape=jax.ShapeDtypeStruct(spectrum.shape, spectrum.dtype),
    )(*operands)


def body(right_side, kappa):
    steps_dev, rows, cols = right_side.shape
    tiles = lax.axis_size("tm")
    total = steps_dev * tiles
    half = total // 2
    margin = HALO
    span = cols // tiles
    width = span + 2 * margin
    tile = lax.axis_index("tm")
    highest = lax.Precision.HIGHEST
    forward, inverse = transform_matrices(total)

    wide_side, kappa_rows, inside_rows = with_halo(right_side, kappa, margin)
    extended = rows + 2 * margin
    lane = 128
    sent = column_tiles(wide_side, tiles, width, margin).reshape(tiles, -1, lane)
    gathered = lax.all_to_all(sent, "tm", 0, 0, tiled=True).reshape(tiles, extended * width)
    spectrum = jnp.dot(forward, gathered, precision=highest)
    spectrum = spectrum.reshape(2, half, extended, width).transpose(0, 2, 1, 3)
    spectrum = spectrum.reshape(2, extended, half * width)

    place = tile * span - margin + jnp.arange(width)
    inside_cols = (place >= 0) & (place < cols)
    inside = inside_rows[:, None] & inside_cols[None, :]
    inside = jnp.tile(inside, (1, half))
    faces = tuple(jnp.tile(f, (1, half)) for f in tile_faces(kappa_rows, tile, tiles, width, margin))
    shifts = slot_shifts(half, total, width)
    solved = solve_slots(spectrum, faces, shifts, inside)

    solved = solved.reshape(2, extended, half, width)[:, margin : margin + rows, :, margin : margin + span]
    signal = jnp.einsum("tks,krsc->trc", inverse.reshape(total, 2, half), solved, precision=highest)
    signal = signal.reshape(total, -1, lane)
    returned = lax.all_to_all(signal, "tm", 0, 0, tiled=True)
    returned = returned.reshape(tiles, rows, span).transpose(1, 0, 2)
    return returned.reshape(steps_dev, rows, cols)


def solution(mesh):
    placed = (P("tm", "row", None), P("row", None))
    return jax.shard_map(
        body, mesh=mesh, in_specs=placed, out_specs=P("tm", "row", None), check_vma=False
    )
```
